32 devices in a mesh: groups: 2 (over y), ctx: 4 (over z), head: 2 (over x), rep: 2 (over core).
Axes of the slice: x: 2, y: 2, z: 4, core: 2. Of those that a mesh axis runs over, the one named last changes fastest.
Arguments:
- queries: bfloat16 [4, 512, 1024], P(('groups', 'rep'), 'ctx', 'head'), parts along dimension 0, may hold values from -6 to 6
- per_head_keys: bfloat16 [4, 512, 1024], P(('groups', 'rep'), 'ctx', 'head'), parts along dimension 0, may hold values from -6 to 6
- value_rows: bfloat16 [4, 512, 1024], P(('groups', 'rep'), 'ctx', 'head'), parts along dimension 0, may hold values from -6 to 6
- gate_logits: bfloat16 [4, 512, 1024], P(('groups', 'rep'), 'ctx', 'head'), parts along dimension 0, may hold values from -16 to 4
- gate_bias: float32 [1024], P('head'), may hold values from -1 to 13
- value_weight: float32 [1024], P('head'), may hold values from -0.1875 to 0.1875
- targets: float32 [4, 512], P(('groups', 'rep'), 'ctx'), parts along dimension 0, may hold values from -6 to 6
- mask_ids: int32 [4, 4], P(('groups', 'rep'), 'ctx'), parts along dimension 0, may hold values from 0 to 3
- segment_starts: int32 [4, 512], P(('groups', 'rep'), 'ctx'), parts along dimension 0, may hold values 0 or 1
Outputs:
- value_pred: float32 [4, 512], P(('groups', 'rep'), 'ctx'), parts along dimension 0
- query_gradient_rows: bfloat16 [4, 512, 1024], P(('groups', 'rep'), 'ctx', 'head'), parts along dimension 0
- grad_keys: bfloat16 [4, 512, 1024], P(('groups', 'rep'), 'ctx', 'head'), parts along dimension 0
- grad_values: bfloat16 [4, 512, 1024], P(('groups', 'rep'), 'ctx', 'head'), parts along dimension 0
- grad_gate_logits: bfloat16 [4, 512, 1024], P(('groups', 'rep'), 'ctx', 'head'), parts along dimension 0
- grad_gate_bias: float32 [2048], P(('groups', 'head')), parts along dimension 0
- grad_value_weight: float32 [2048], P(('groups', 'head')), parts along dimension 0
The draws below stay inside these ranges and needn't reach their ends.
There are 2 independent parts, one for each index of `groups`. The reference program is written for one: setup_inputs(seed, part) draws one part's arguments, and reference() takes and returns one part's arrays. A program takes and returns all parts, laid end to end along the dimension named above; an argument that names none is the same for every part. Nothing has to cross between parts.
Inputs may be any that keep to these rules, and one draw needn't show every extreme that they name: `mask_ids`: the window kind of each block of 128 positions. `segment_starts`: flags of segment starts.
All inputs are finite; a program needn't handle non-finite values. No bound on the sum of `segment_starts` on one device may be relied on, other than what follows from the above.
Results may differ from the reference program's by a relative error of at most 0.013.
Values sent between devices are 32-bit elements; how exact they have to be, the bound alone decides.
No kernel may reach another device: no remote copies, remote signals or barrier semaphores. Data moves between devices by JAX's collectives and lax.ppermute only.
A program may use at most 64 MiB of HBM per device.

```python
import jax
import jax.numpy as jnp
from jax import lax

DK = 128
DV = 128
BLOCK = 128
TOK_DEV = 128
HEADS = 8
SEQUENCE_LENGTH = 512
SEQUENCE_GROUP = 2


def draw_gate_logits(key, part):
    first, latter_half, third = jax.random.split(key, 3)
    shape = (SEQUENCE_GROUP, SEQUENCE_LENGTH, HEADS * DK)
    start_offset = jnp.clip(jax.random.normal(first, shape, jnp.float32), -4.0, 4.0)
    position_span = jax.random.bernoulli(latter_half, 1.0 / 1024.0, (SEQUENCE_GROUP, SEQUENCE_LENGTH, 1))
    level_number = jax.random.uniform(third, (SEQUENCE_GROUP, SEQUENCE_LENGTH, 1), jnp.float32, -16.0, -12.0)
    return jnp.where(position_span, level_number, start_offset).astype(jnp.bfloat16)


def draw_gate_bias(key, part):
    first = jax.random.fold_in(key, 0)
    return jax.random.uniform(first, (HEADS * DK,), jnp.float32, -1.0, 13.0)


def with_ends(values, own_key, low, top_value):
    index_at = [jax.random.randint(jax.random.fold_in(own_key, axis), (), 0, length) for axis, length in enumerate(values.shape)]
    longest = values.shape.index(max(values.shape))
    neighbour = index_at[:longest] + [(index_at[longest] + 1) % values.shape[longest]] + index_at[longest + 1:]
    return values.at[tuple(index_at)].set(low).at[tuple(neighbour)].set(top_value)


def block_levels(key, dims, cuts, least, largest):
    gain, own = 1.0, jax.random.fold_in(key, 6)
    for axis_at, blocks in cuts:
        steps = jnp.exp(jax.random.uniform(jax.random.fold_in(own, axis_at), (blocks,), jnp.float32, least / len(cuts), largest / len(cuts)))
        gain = gain * jnp.repeat(steps, dims[axis_at] // blocks).reshape([-1 if axis == axis_at else 1 for axis in range(len(dims))])
    return gain


def scatter_about(stream_key, extent, spread, most, cuts=(), kind=jnp.bfloat16):
    drawn = jax.random.normal(stream_key, extent, jnp.float32) * spread
    if len(cuts) > 0:
        drawn = block_levels(stream_key, extent, cuts, -0.22, 0.18) * drawn
    return jnp.clip(drawn, min=-most, max=most).astype(kind)


def setup_inputs(seed: int = 0, part: int = 0) -> dict:
    key_list = jax.random.split(jax.random.key(seed), 10)
    own_keys = jax.random.split(jax.random.fold_in(key_list[9], part), 10)
    return {
        "queries": scatter_about(own_keys[0], (SEQUENCE_GROUP, SEQUENCE_LENGTH, HEADS * DK), 1.0, 6.0, ((0, 2), (1, 4), (2, 2))),
        "per_head_keys": scatter_about(own_keys[1], (SEQUENCE_GROUP, SEQUENCE_LENGTH, HEADS * DK), 1.0, 6.0, ((0, 2), (1, 4), (2, 2))),
        "value_rows": scatter_about(own_keys[2], (SEQUENCE_GROUP, SEQUENCE_LENGTH, HEADS * DV), 1.0, 6.0, ((0, 2), (1, 4), (2, 2))),
        "gate_logits": draw_gate_logits(jax.random.fold_in(jax.random.fold_in(key_list[9], part), 71), part),
        "gate_bias": draw_gate_bias(jax.random.fold_in(key_list[9], 71), part),
        "value_weight": scatter_about(key_list[5], (HEADS * DV,), (HEADS * DV) ** -0.5, 0.1875, ((0, 2),), jnp.float32),
        "targets": scatter_about(own_keys[6], (SEQUENCE_GROUP, SEQUENCE_LENGTH), 1.0, 6.0, ((0, 2), (1, 4)), jnp.float32),
        "mask_ids": with_ends(jax.random.randint(own_keys[7], (SEQUENCE_GROUP, SEQUENCE_LENGTH // BLOCK), 0, 4), jax.random.fold_in(own_keys[7], 1), 0, 3).astype(jnp.int32),
        "segment_starts": with_ends((jax.random.randint(own_keys[8], (SEQUENCE_GROUP, SEQUENCE_LENGTH), 0, 4 * TOK_DEV) < 1).astype(jnp.int32), jax.random.fold_in(own_keys[8], 1), 0, 1),
    }


epsilon = 1.0
gate_scale = 16.0
highest = lax.Precision.HIGHEST

def block_pass(query_in, key_in, value_in, decay, start_flags, kind_ids):
    blocks = kind_ids.shape[0]
    block_len = query_in.shape[0] // blocks
    head_count = query_in.shape[1]
    channels = query_in.shape[2]
    value_width = value_in.shape[2]
    query_f = query_in.astype(jnp.float32).reshape(blocks, block_len, head_count, channels)
    key_f = key_in.astype(jnp.float32).reshape(blocks, block_len, head_count, channels)
    value_f = value_in.astype(jnp.float32).reshape(blocks, block_len, head_count, value_width)
    log_cum = jnp.cumsum(decay.reshape(blocks, block_len, head_count, channels), axis=1)
    log_last = log_cum[:, -1]
    segment = jnp.cumsum(start_flags.reshape(blocks, block_len), axis=1, dtype=jnp.int32)
    alive_mask = (segment == 0).astype(jnp.float32)
    offsets = jnp.arange(block_len, dtype=jnp.int32)
    distance = offsets[:, None] - offsets[None, :]
    window = block_len // jnp.left_shift(jnp.ones_like(kind_ids), kind_ids)
    live_pairs = (segment[:, :, None] == segment[:, None, :]) & (distance[None] >= 0) & (distance[None] < window[:, None, None])
    query_dec = query_f * jnp.exp(log_cum) * channels ** (-0.5)
    key_dec = key_f * jnp.exp(-log_cum)
    scores = jnp.einsum('bihc,bjhc->bhij', query_dec, key_dec, precision=highest)
    block_probs = jnp.where(live_pairs[:, None], scores, 0.0).astype(jnp.bfloat16)
    inner_part = jnp.einsum('bhij,bjhd->bihd', block_probs.astype(jnp.float32), value_f, precision=highest)
    tail_mask = (segment == segment[:, -1:]).astype(jnp.float32)
    key_tail = key_f * jnp.exp(log_last[:, None] - log_cum) * tail_mask[:, :, None, None]
    block_state = jnp.einsum('bjhc,bjhd->bhcd', key_tail, value_f, precision=highest)
    block_decay = jnp.exp(log_last) * alive_mask[:, -1][:, None, None]

    def advance(carried_in, block_items):
        state_now, factor = carried_in
        new_state = state_now * block_items[1][..., None] + block_items[0]
        return ((new_state, factor * block_items[1]), (state_now, factor))
    initial = (jnp.zeros((head_count, channels, value_width), jnp.float32), jnp.ones((head_count, channels), jnp.float32))
    finals, befores = lax.scan(advance, initial, (block_state, block_decay))
    query_live = query_dec * alive_mask[:, :, None, None]
    outer_part = jnp.einsum('bihc,bhcd->bihd', query_live, befores[0], precision=highest)
    carried = query_live * befores[1][:, None]
    attended = (inner_part + outer_part).reshape(blocks * block_len, head_count, value_width)
    return (attended, finals[0], finals[1], carried.reshape(blocks * block_len, head_count, channels))

def head_forward(query_in, key_in, value_in, logit_in, bias_in, weight_in, segment_starts, mask_ids):

    def one_sequence(query_seq, key_seq, value_seq, logit_seq, start_seq, kind_seq):
        decay = jax.nn.log_sigmoid(logit_seq.astype(jnp.float32) + bias_in) / gate_scale
        attended = block_pass(query_seq[:, None], key_seq[:, None], value_seq[:, None], decay[:, None], start_seq, kind_seq)[0][:, 0]
        normed = attended * lax.rsqrt(lax.optimization_barrier(jnp.mean(attended * attended, axis=-1, keepdims=True)) + epsilon)
        return jnp.dot(normed, weight_in, precision=highest)
    return jax.vmap(one_sequence)(query_in, key_in, value_in, logit_in, segment_starts, mask_ids)

def reference(queries, per_head_keys, value_rows, gate_logits, gate_bias, value_weight, targets, mask_ids, segment_starts):
    sequence_count, length, feature_count = queries.shape

    def split_heads(array):
        return array.reshape(sequence_count, length, HEADS, -1).transpose(2, 0, 1, 3)

    def merge_heads(array):
        return array.transpose(1, 2, 0, 3).reshape(sequence_count, length, -1)
    per_head = (split_heads(queries), split_heads(per_head_keys), split_heads(value_rows), split_heads(gate_logits), gate_bias.reshape(HEADS, DK), value_weight.reshape(HEADS, DV))

    def forward_only(items):
        return head_forward(*items, segment_starts, mask_ids)
    value_pred = lax.optimization_barrier(jnp.sum(lax.map(forward_only, per_head), axis=0))
    residual = value_pred - targets

    def backward_head(items):

        def head_value(*inputs):
            return head_forward(*inputs, segment_starts, mask_ids)
        unused, pull = jax.vjp(head_value, *items)
        return pull(residual)
    grads = lax.map(backward_head, per_head)
    token_total = sequence_count * length
    return (value_pred, merge_heads(grads[0]), merge_heads(grads[1]), merge_heads(grads[2]), merge_heads(grads[3]), grads[4].reshape(-1) / token_total, grads[5].reshape(-1) / token_total)
```

```python
import jax
import jax.numpy as jnp
from jax import lax
from jax.sharding import PartitionSpec as P

DK = 128
DV = 128


epsilon = 1.0
gate_scale = 16.0
highest = lax.Precision.HIGHEST


def from_behind(value, axis, by):
    length = lax.axis_size(axis)
    pairs = [(i, i + by) for i in range(length) if 0 <= i + by < length]
    return lax.ppermute(value, axis, pairs)


def pack_state(state, factor):
    rows = jnp.zeros((state.shape[0], 8, state.shape[2]), state.dtype)
    rows = rows.at[:, 0, :].set(factor)
    return jnp.concatenate([state, rows], axis=1)


def gather_scan(state, factor, span_count, direction):
    if span_count == 1:
        return jnp.zeros_like(state)
    channels = state.shape[1]
    packed = pack_state(state, factor)
    received = []
    for shift in range(1, span_count):
        payload = packed if shift < span_count - 1 else state
        received.append(from_behind(payload, "ctx", direction * shift))
    total = received[-1][:, :channels]
    for shift in range(span_count - 2, 0, -1):
        part = received[shift - 1]
        total = total * part[:, channels, :][..., None] + part[:, :channels]
    return total


def block_pass(query_in, key_in, value_in, decay, start_flags, kind_ids):
    blocks = kind_ids.shape[0]
    block_len = query_in.shape[0] // blocks
    head_count = query_in.shape[1]
    channels = query_in.shape[2]
    value_width = value_in.shape[2]
    query_f = query_in.astype(jnp.float32).reshape(blocks, block_len, head_count, channels)
    key_f = key_in.astype(jnp.float32).reshape(blocks, block_len, head_count, channels)
    value_bf = value_in.reshape(blocks, block_len, head_count, value_width)
    value_f = value_bf.astype(jnp.float32)
    log_cum = jnp.cumsum(decay.reshape(blocks, block_len, head_count, channels), axis=1)
    log_last = log_cum[:, -1]
    segment = jnp.cumsum(start_flags.reshape(blocks, block_len), axis=1, dtype=jnp.int32)
    alive_mask = (segment == 0).astype(jnp.float32)
    offsets = jnp.arange(block_len, dtype=jnp.int32)
    distance = offsets[:, None] - offsets[None, :]
    window = block_len // jnp.left_shift(jnp.ones_like(kind_ids), kind_ids)
    live_pairs = (
        (segment[:, :, None] == segment[:, None, :])
        & (distance[None] >= 0)
        & (distance[None] < window[:, None, None])
    )
    query_dec = query_f * jnp.exp(log_cum) * channels ** (-0.5)
    key_dec = key_f * jnp.exp(-log_cum)
    scores = jnp.einsum("bihc,bjhc->bhij", query_dec, key_dec, precision=highest)
    block_probs = jnp.where(live_pairs[:, None], scores, 0.0).astype(jnp.bfloat16)
    inner_part = jnp.einsum(
        "bhij,bjhd->bihd", block_probs, value_bf, preferred_element_type=jnp.float32
    )
    tail_mask = (segment == segment[:, -1:]).astype(jnp.float32)
    key_tail = key_f * jnp.exp(log_last[:, None] - log_cum) * tail_mask[:, :, None, None]
    block_state = jnp.einsum("bjhc,bjhd->bhcd", key_tail, value_f, precision=highest)
    block_decay = jnp.exp(log_last) * alive_mask[:, -1][:, None, None]

    def advance(carried_in, block_items):
        state_now, factor = carried_in
        new_state = state_now * block_items[1][..., None] + block_items[0]
        return ((new_state, factor * block_items[1]), (state_now, factor))

    initial = (
        jnp.zeros((head_count, channels, value_width), jnp.float32),
        jnp.ones((head_count, channels), jnp.float32),
    )
    finals, befores = lax.scan(advance, initial, (block_state, block_decay))
    query_live = query_dec * alive_mask[:, :, None, None]
    outer_part = jnp.einsum("bihc,bhcd->bihd", query_live, befores[0], precision=highest)
    carried = query_live * befores[1][:, None]
    attended = (inner_part + outer_part).reshape(blocks * block_len, head_count, value_width)
    return (
        attended,
        finals[0],
        finals[1],
        carried.reshape(blocks * block_len, head_count, channels),
    )


def on_device(
    queries,
    per_head_keys,
    value_rows,
    gate_logits,
    gate_bias,
    value_weight,
    targets,
    mask_ids,
    segment_starts,
):
    token_count = queries.shape[1]
    head_count = gate_bias.shape[0] // DK

    def to_heads(array):
        return array[0].reshape(token_count, head_count, -1)

    start_flags = segment_starts[0]
    kind_ids = mask_ids[0]

    def local_terms(query_in, key_in, value_in, logit_in, bias_in):
        decay = jax.nn.log_sigmoid(logit_in.astype(jnp.float32) + bias_in) / gate_scale
        return block_pass(query_in, key_in, value_in, decay, start_flags, kind_ids)

    local_out, pull_local = jax.vjp(
        local_terms,
        to_heads(queries),
        to_heads(per_head_keys),
        to_heads(value_rows),
        to_heads(gate_logits),
        gate_bias.reshape(head_count, DK),
    )
    attended_local, state_local, decay_local, carried = local_out

    span_count = lax.axis_size("ctx")
    state_in = gather_scan(state_local, decay_local, span_count, 1)
    attended = attended_local + jnp.einsum("thc,hcd->thd", carried, state_in, precision=highest)

    def value_head(attended_in, weight_in):
        normed = attended_in * lax.rsqrt(
            jnp.mean(attended_in * attended_in, axis=-1, keepdims=True) + epsilon
        )
        return jnp.einsum("thd,hd->t", normed, weight_in, precision=highest)

    partial_value, pull_value = jax.vjp(value_head, attended, value_weight.reshape(head_count, DV))
    value_pred = lax.psum(partial_value, "head")
    residual = value_pred - targets[0]
    grad_attended, grad_weight = pull_value(residual)
    grad_carried = jnp.einsum("thd,hcd->thc", grad_attended, state_in, precision=highest)
    grad_direct = jnp.einsum("thc,thd->hcd", carried, grad_attended, precision=highest)

    grad_state = gather_scan(grad_direct, decay_local, span_count, -1)
    grad_decay = jnp.sum(state_in * grad_state, axis=-1)
    grad_query, grad_key, grad_value, grad_logit, grad_bias = pull_local(
        (grad_attended, grad_state, grad_decay, grad_carried)
    )
    token_total = token_count * lax.axis_size("ctx") * lax.axis_size("rep")
    bias_total, weight_total = lax.psum(
        (grad_bias.reshape(-1), grad_weight.reshape(-1)), ("ctx", "rep")
    )
    return (
        value_pred[None],
        grad_query.reshape(1, token_count, -1),
        grad_key.reshape(1, token_count, -1),
        grad_value.reshape(1, token_count, -1),
        grad_logit.reshape(1, token_count, -1),
        bias_total / token_total,
        weight_total / token_total,
    )


def solution(mesh):
    in_specs = (
        P(("groups", "rep"), "ctx", "head"),
        P(("groups", "rep"), "ctx", "head"),
        P(("groups", "rep"), "ctx", "head"),
        P(("groups", "rep"), "ctx", "head"),
        P("head"),
        P("head"),
        P(("groups", "rep"), "ctx"),
        P(("groups", "rep"), "ctx"),
        P(("groups", "rep"), "ctx"),
    )
    out_specs = (
        P(("groups", "rep"), "ctx"),
        P(("groups", "rep"), "ctx", "head"),
        P(("groups", "rep"), "ctx", "head"),
        P(("groups", "rep"), "ctx", "head"),
        P(("groups", "rep"), "ctx", "head"),
        P(("groups", "head")),
        P(("groups", "head")),
    )
    return jax.shard_map(
        on_device, mesh=mesh, in_specs=in_specs, out_specs=out_specs, check_vma=False
    )
```

```python
import jax
import jax.numpy as jnp
from jax import lax
from jax.sharding import PartitionSpec as P

DK = 128
DV = 128


epsilon = 1.0
gate_scale = 16.0
highest = lax.Precision.HIGHEST


def from_behind(value, axis, by):
    length = lax.axis_size(axis)
    pairs = [(i, i + by) for i in range(length) if 0 <= i + by < length]
    return lax.ppermute(value, axis, pairs)


def pack_state(state, factor):
    rows = jnp.zeros((state.shape[0], 8, state.shape[2]), state.dtype)
    rows = rows.at[:, 0, :].set(factor)
    return jnp.concatenate([state, rows], axis=1)


def gather_scan(state, factor, span_count, direction):
    if span_count == 1:
        return jnp.zeros_like(state)
    channels = state.shape[1]
    packed = pack_state(state, factor)
    received = []
    for shift in range(1, span_count):
        payload = packed if shift < span_count - 1 else state
        received.append(from_behind(payload, "ctx", direction * shift))
    total = received[-1][:, :channels]
    for shift in range(span_count - 2, 0, -1):
        part = received[shift - 1]
        total = total * part[:, channels, :][..., None] + part[:, :channels]
    return total


def log_decay(logit_in, bias_in):
    return jax.nn.log_sigmoid(logit_in + bias_in) / gate_scale


def segment_ids(start_flags):
    return jnp.cumsum(start_flags, axis=0, dtype=jnp.int32)


def block_inner(query_in, key_in, value_in, logit_in, bias_in, start_flags, kind_id):
    block_len = query_in.shape[0]
    channels = query_in.shape[2]
    log_cum = jnp.cumsum(log_decay(logit_in, bias_in), axis=0)
    segment = segment_ids(start_flags)
    alive_mask = (segment == 0).astype(jnp.float32)
    offsets = jnp.arange(block_len, dtype=jnp.int32)
    distance = offsets[:, None] - offsets[None, :]
    window = block_len // jnp.left_shift(jnp.ones_like(kind_id), kind_id)
    live_pairs = (
        (segment[:, None] == segment[None, :]) & (distance >= 0) & (distance < window)
    )
    query_dec = query_in * jnp.exp(log_cum) * channels ** (-0.5)
    key_dec = key_in * jnp.exp(-log_cum)
    scores = jnp.einsum("ihc,jhc->hij", query_dec, key_dec, precision=highest)
    block_probs = jnp.where(live_pairs[None], scores, 0.0).astype(jnp.bfloat16)
    inner_part = jnp.einsum(
        "hij,jhd->ihd",
        block_probs,
        value_in.astype(jnp.bfloat16),
        preferred_element_type=jnp.float32,
    )
    carried = query_dec * alive_mask[:, None, None]
    return inner_part, carried


def block_summary(key_in, value_in, logit_in, bias_in, start_flags):
    log_cum = jnp.cumsum(log_decay(logit_in, bias_in), axis=0)
    log_last = log_cum[-1]
    segment = segment_ids(start_flags)
    alive_last = (segment[-1] == 0).astype(jnp.float32)
    tail_mask = (segment == segment[-1]).astype(jnp.float32)
    key_tail = key_in * jnp.exp(log_last[None] - log_cum) * tail_mask[:, None, None]
    block_state = jnp.einsum("jhc,jhd->hcd", key_tail, value_in, precision=highest)
    block_decay = jnp.exp(log_last) * alive_last
    return block_state, block_decay


def on_device(
    queries,
    per_head_keys,
    value_rows,
    gate_logits,
    gate_bias,
    value_weight,
    targets,
    mask_ids,
    segment_starts,
):
    token_count = queries.shape[1]
    head_count = gate_bias.shape[0] // DK
    assert mask_ids.shape[1] == 1

    def to_heads(array):
        return array[0].reshape(token_count, head_count, -1).astype(jnp.float32)

    start_flags = segment_starts[0]
    kind_id = mask_ids[0, 0]
    query_f = to_heads(queries)
    key_f = to_heads(per_head_keys)
    value_f = to_heads(value_rows)
    logit_f = to_heads(gate_logits)
    bias_h = gate_bias.reshape(head_count, DK)

    def inner_terms(query_in, key_in, value_in, logit_in, bias_in):
        return block_inner(query_in, key_in, value_in, logit_in, bias_in, start_flags, kind_id)

    def summary_terms(key_in, value_in, logit_in, bias_in):
        return block_summary(key_in, value_in, logit_in, bias_in, start_flags)

    (attended_local, carried), pull_inner = jax.vjp(
        inner_terms, query_f, key_f, value_f, logit_f, bias_h
    )
    (state_local, decay_local), pull_summary = jax.vjp(
        summary_terms, key_f, value_f, logit_f, bias_h
    )

    span_count = lax.axis_size("ctx")
    state_in = gather_scan(state_local, decay_local, span_count, 1)
    attended = attended_local + jnp.einsum("thc,hcd->thd", carried, state_in, precision=highest)

    def value_head(attended_in, weight_in):
        normed = attended_in * lax.rsqrt(
            jnp.mean(attended_in * attended_in, axis=-1, keepdims=True) + epsilon
        )
        return jnp.einsum("thd,hd->t", normed, weight_in, precision=highest)

    partial_value, pull_value = jax.vjp(value_head, attended, value_weight.reshape(head_count, DV))
    value_pred = lax.psum(partial_value, "head")
    residual = value_pred - targets[0]
    grad_attended, grad_weight = pull_value(residual)
    grad_carried = jnp.einsum("thd,hcd->thc", grad_attended, state_in, precision=highest)
    grad_direct = jnp.einsum("thc,thd->hcd", carried, grad_attended, precision=highest)
    inner_grads = pull_inner((grad_attended, grad_carried))

    grad_state = gather_scan(grad_direct, decay_local, span_count, -1)
    grad_decay = jnp.sum(state_in * grad_state, axis=-1)
    summary_grads = pull_summary((grad_state, grad_decay))

    grad_query = inner_grads[0]
    grad_key = inner_grads[1] + summary_grads[0]
    grad_value = inner_grads[2] + summary_grads[1]
    grad_logit = inner_grads[3] + summary_grads[2]
    grad_bias = inner_grads[4] + summary_grads[3]
    token_total = token_count * lax.axis_size("ctx") * lax.axis_size("rep")
    bias_total, weight_total = lax.psum(
        (grad_bias.reshape(-1), grad_weight.reshape(-1)), ("ctx", "rep")
    )

    def to_rows(array):
        return array.reshape(1, token_count, -1).astype(jnp.bfloat16)

    return (
        value_pred[None],
        to_rows(grad_query),
        to_rows(grad_key),
        to_rows(grad_value),
        to_rows(grad_logit),
        bias_total / token_total,
        weight_total / token_total,
    )


def solution(mesh):
    in_specs = (
        P(("groups", "rep"), "ctx", "head"),
        P(("groups", "rep"), "ctx", "head"),
        P(("groups", "rep"), "ctx", "head"),
        P(("groups", "rep"), "ctx", "head"),
        P("head"),
        P("head"),
        P(("groups", "rep"), "ctx"),
        P(("groups", "rep"), "ctx"),
        P(("groups", "rep"), "ctx"),
    )
    out_specs = (
        P(("groups", "rep"), "ctx"),
        P(("groups", "rep"), "ctx", "head"),
        P(("groups", "rep"), "ctx", "head"),
        P(("groups", "rep"), "ctx", "head"),
        P(("groups", "rep"), "ctx", "head"),
        P(("groups", "head")),
        P(("groups", "head")),
    )
    return jax.shard_map(
        on_device, mesh=mesh, in_specs=in_specs, out_specs=out_specs, check_vma=False
    )
```

```python
import jax
import jax.numpy as jnp
from jax import lax
from jax.sharding import PartitionSpec as P

DK = 128
DV = 128


epsilon = 1.0
gate_scale = 16.0
highest = lax.Precision.HIGHEST


def from_behind(value, axis, by):
    length = lax.axis_size(axis)
    pairs = [(i, i + by) for i in range(length) if 0 <= i + by < length]
    return lax.ppermute(value, axis, pairs)


def pack_state(state, factor):
    rows = jnp.zeros((state.shape[0], 8, state.shape[2]), state.dtype)
    rows = rows.at[:, 0, :].set(factor)
    return jnp.concatenate([state, rows], axis=1)


def gather_scan(state, factor, span_count, direction):
    channels = state.shape[1]
    near_a, near_b = None, None
    run_a, run_b = state, factor
    shift = 1
    while shift < span_count:
        last = 2 * shift >= span_count
        if last:
            far = from_behind(run_a, "ctx", direction * shift)
            far_a, far_b = far, None
        else:
            far = from_behind(pack_state(run_a, factor=run_b), "ctx", direction * shift)
            far_a, far_b = far[:, :channels], far[:, channels, :]
        if near_a is None:
            near_a, near_b = far_a, far_b
        else:
            near_a = far_a * near_b[..., None] + near_a
            near_b = None if last else far_b * near_b
        if not last:
            run_a = far_a * run_b[..., None] + run_a
            run_b = far_b * run_b
        shift *= 2
    if near_a is None:
        return jnp.zeros_like(state)
    return near_a


def log_decay(logit_in, bias_in):
    return jax.nn.log_sigmoid(logit_in + bias_in) / gate_scale


def segment_ids(start_flags):
    return jnp.cumsum(start_flags, axis=0, dtype=jnp.int32)


def block_inner(query_in, key_in, value_in, logit_in, bias_in, start_flags, kind_id):
    block_len = query_in.shape[0]
    channels = query_in.shape[2]
    log_cum = jnp.cumsum(log_decay(logit_in, bias_in), axis=0)
    segment = segment_ids(start_flags)
    alive_mask = (segment == 0).astype(jnp.float32)
    offsets = jnp.arange(block_len, dtype=jnp.int32)
    distance = offsets[:, None] - offsets[None, :]
    window = block_len // jnp.left_shift(jnp.ones_like(kind_id), kind_id)
    live_pairs = (
        (segment[:, None] == segment[None, :]) & (distance >= 0) & (distance < window)
    )
    query_dec = query_in * jnp.exp(log_cum) * channels ** (-0.5)
    key_dec = key_in * jnp.exp(-log_cum)
    scores = jnp.einsum("ihc,jhc->hij", query_dec, key_dec, precision=highest)
    block_probs = jnp.where(live_pairs[None], scores, 0.0).astype(jnp.bfloat16)
    inner_part = jnp.einsum(
        "hij,jhd->ihd",
        block_probs,
        value_in.astype(jnp.bfloat16),
        preferred_element_type=jnp.float32,
    )
    carried = query_dec * alive_mask[:, None, None]
    return inner_part, carried


def block_summary(key_in, value_in, logit_in, bias_in, start_flags):
    log_cum = jnp.cumsum(log_decay(logit_in, bias_in), axis=0)
    log_last = log_cum[-1]
    segment = segment_ids(start_flags)
    alive_last = (segment[-1] == 0).astype(jnp.float32)
    tail_mask = (segment == segment[-1]).astype(jnp.float32)
    key_tail = key_in * jnp.exp(log_last[None] - log_cum) * tail_mask[:, None, None]
    block_state = jnp.einsum("jhc,jhd->hcd", key_tail, value_in, precision=highest)
    block_decay = jnp.exp(log_last) * alive_last
    return block_state, block_decay


def on_device(
    queries,
    per_head_keys,
    value_rows,
    gate_logits,
    gate_bias,
    value_weight,
    targets,
    mask_ids,
    segment_starts,
):
    token_count = queries.shape[1]
    head_count = gate_bias.shape[0] // DK
    assert mask_ids.shape[1] == 1

    def to_heads(array):
        return array[0].reshape(token_count, head_count, -1).astype(jnp.float32)

    start_flags = segment_starts[0]
    kind_id = mask_ids[0, 0]
    query_f = to_heads(queries)
    key_f = to_heads(per_head_keys)
    value_f = to_heads(value_rows)
    logit_f = to_heads(gate_logits)
    bias_h = gate_bias.reshape(head_count, DK)

    def inner_terms(query_in, key_in, value_in, logit_in, bias_in):
        return block_inner(query_in, key_in, value_in, logit_in, bias_in, start_flags, kind_id)

    def summary_terms(key_in, value_in, logit_in, bias_in):
        return block_summary(key_in, value_in, logit_in, bias_in, start_flags)

    (attended_local, carried), pull_inner = jax.vjp(
        inner_terms, query_f, key_f, value_f, logit_f, bias_h
    )
    (state_local, decay_local), pull_summary = jax.vjp(
        summary_terms, key_f, value_f, logit_f, bias_h
    )

    span_count = lax.axis_size("ctx")
    state_in = gather_scan(state_local, decay_local, span_count, 1)
    attended = attended_local + jnp.einsum("thc,hcd->thd", carried, state_in, precision=highest)

    def value_head(attended_in, weight_in):
        normed = attended_in * lax.rsqrt(
            jnp.mean(attended_in * attended_in, axis=-1, keepdims=True) + epsilon
        )
        return jnp.einsum("thd,hd->t", normed, weight_in, precision=highest)

    partial_value, pull_value = jax.vjp(value_head, attended, value_weight.reshape(head_count, DV))
    value_pred = lax.psum(partial_value, "head")
    residual = value_pred - targets[0]
    grad_attended, grad_weight = pull_value(residual)
    grad_carried = jnp.einsum("thd,hcd->thc", grad_attended, state_in, precision=highest)
    grad_direct = jnp.einsum("thc,thd->hcd", carried, grad_attended, precision=highest)
    inner_grads = pull_inner((grad_attended, grad_carried))

    grad_state = gather_scan(grad_direct, decay_local, span_count, -1)
    grad_decay = jnp.sum(state_in * grad_state, axis=-1)
    summary_grads = pull_summary((grad_state, grad_decay))

    grad_query = inner_grads[0]
    grad_key = inner_grads[1] + summary_grads[0]
    grad_value = inner_grads[2] + summary_grads[1]
    grad_logit = inner_grads[3] + summary_grads[2]
    grad_bias = inner_grads[4] + summary_grads[3]
    token_total = token_count * lax.axis_size("ctx") * lax.axis_size("rep")
    bias_total, weight_total = lax.psum(
        (grad_bias.reshape(-1), grad_weight.reshape(-1)), ("ctx", "rep")
    )

    def to_rows(array):
        return array.reshape(1, token_count, -1).astype(jnp.bfloat16)

    return (
        value_pred[None],
        to_rows(grad_query),
        to_rows(grad_key),
        to_rows(grad_value),
        to_rows(grad_logit),
        bias_total / token_total,
        weight_total / token_total,
    )


def solution(mesh):
    in_specs = (
        P(("groups", "rep"), "ctx", "head"),
        P(("groups", "rep"), "ctx", "head"),
        P(("groups", "rep"), "ctx", "head"),
        P(("groups", "rep"), "ctx", "head"),
        P("head"),
        P("head"),
        P(("groups", "rep"), "ctx"),
        P(("groups", "rep"), "ctx"),
        P(("groups", "rep"), "ctx"),
    )
    out_specs = (
        P(("groups", "rep"), "ctx"),
        P(("groups", "rep"), "ctx", "head"),
        P(("groups", "rep"), "ctx", "head"),
        P(("groups", "rep"), "ctx", "head"),
        P(("groups", "rep"), "ctx", "head"),
        P(("groups", "head")),
        P(("groups", "head")),
    )
    return jax.shard_map(
        on_device, mesh=mesh, in_specs=in_specs, out_specs=out_specs, check_vma=False
    )
```

```python
import jax
import jax.numpy as jnp
from jax import lax
from jax.sharding import PartitionSpec as P

DK = 128
DV = 128


epsilon = 1.0
gate_scale = 16.0
highest = lax.Precision.HIGHEST


def from_behind(value, axis, by):
    length = lax.axis_size(axis)
    pairs = [(i, i + by) for i in range(length) if 0 <= i + by < length]
    return lax.ppermute(value, axis, pairs)


def butterfly_sum(value, axis):
    length = lax.axis_size(axis)
    if length & (length - 1):
        return lax.psum(value, axis)
    bit = 1
    while bit < length:
        pairs = [(i, i ^ bit) for i in range(length)]
        value = value + lax.ppermute(value, axis, pairs)
        bit *= 2
    return value


def pack_state(state, factor):
    rows = jnp.zeros((state.shape[0], 8, state.shape[2]), state.dtype)
    rows = rows.at[:, 0, :].set(factor)
    return jnp.concatenate([state, rows], axis=1)


def gather_scan(state, factor, span_count, direction):
    channels = state.shape[1]
    near_a, near_b = None, None
    run_a, run_b = state, factor
    shift = 1
    while shift < span_count:
        last = 2 * shift >= span_count
        if last:
            far = from_behind(run_a, "ctx", direction * shift)
            far_a, far_b = far, None
        else:
            far = from_behind(pack_state(run_a, factor=run_b), "ctx", direction * shift)
            far_a, far_b = far[:, :channels], far[:, channels, :]
        if near_a is None:
            near_a, near_b = far_a, far_b
        else:
            near_a = far_a * near_b[..., None] + near_a
            near_b = None if last else far_b * near_b
        if not last:
            run_a = far_a * run_b[..., None] + run_a
            run_b = far_b * run_b
        shift *= 2
    if near_a is None:
        return jnp.zeros_like(state)
    return near_a


def log_decay(logit_in, bias_in):
    return jax.nn.log_sigmoid(logit_in + bias_in) / gate_scale


def segment_ids(start_flags):
    return jnp.cumsum(start_flags, axis=0, dtype=jnp.int32)


def block_inner(query_in, key_in, value_in, logit_in, bias_in, start_flags, kind_id):
    block_len = query_in.shape[0]
    channels = query_in.shape[2]
    log_cum = jnp.cumsum(log_decay(logit_in, bias_in), axis=0)
    segment = segment_ids(start_flags)
    alive_mask = (segment == 0).astype(jnp.float32)
    offsets = jnp.arange(block_len, dtype=jnp.int32)
    distance = offsets[:, None] - offsets[None, :]
    window = block_len // jnp.left_shift(jnp.ones_like(kind_id), kind_id)
    live_pairs = (
        (segment[:, None] == segment[None, :]) & (distance >= 0) & (distance < window)
    )
    query_dec = query_in * jnp.exp(log_cum) * channels ** (-0.5)
    key_dec = key_in * jnp.exp(-log_cum)
    scores = jnp.einsum("ihc,jhc->hij", query_dec, key_dec, precision=highest)
    block_probs = jnp.where(live_pairs[None], scores, 0.0).astype(jnp.bfloat16)
    inner_part = jnp.einsum(
        "hij,jhd->ihd",
        block_probs,
        value_in.astype(jnp.bfloat16),
        preferred_element_type=jnp.float32,
    )
    carried = query_dec * alive_mask[:, None, None]
    return inner_part, carried


def block_summary(key_in, value_in, logit_in, bias_in, start_flags):
    log_cum = jnp.cumsum(log_decay(logit_in, bias_in), axis=0)
    log_last = log_cum[-1]
    segment = segment_ids(start_flags)
    alive_last = (segment[-1] == 0).astype(jnp.float32)
    tail_mask = (segment == segment[-1]).astype(jnp.float32)
    key_tail = key_in * jnp.exp(log_last[None] - log_cum) * tail_mask[:, None, None]
    block_state = jnp.einsum("jhc,jhd->hcd", key_tail, value_in, precision=highest)
    block_decay = jnp.exp(log_last) * alive_last
    return block_state, block_decay


def on_device(
    queries,
    per_head_keys,
    value_rows,
    gate_logits,
    gate_bias,
    value_weight,
    targets,
    mask_ids,
    segment_starts,
):
    token_count = queries.shape[1]
    head_count = gate_bias.shape[0] // DK
    assert mask_ids.shape[1] == 1

    def to_heads(array):
        return array[0].reshape(token_count, head_count, -1).astype(jnp.float32)

    start_flags = segment_starts[0]
    kind_id = mask_ids[0, 0]
    query_f = to_heads(queries)
    key_f = to_heads(per_head_keys)
    value_f = to_heads(value_rows)
    logit_f = to_heads(gate_logits)
    bias_h = gate_bias.reshape(head_count, DK)

    def inner_terms(query_in, key_in, value_in, logit_in, bias_in):
        return block_inner(query_in, key_in, value_in, logit_in, bias_in, start_flags, kind_id)

    def summary_terms(key_in, value_in, logit_in, bias_in):
        return block_summary(key_in, value_in, logit_in, bias_in, start_flags)

    (attended_local, carried), pull_inner = jax.vjp(
        inner_terms, query_f, key_f, value_f, logit_f, bias_h
    )
    (state_local, decay_local), pull_summary = jax.vjp(
        summary_terms, key_f, value_f, logit_f, bias_h
    )

    span_count = lax.axis_size("ctx")
    state_in = gather_scan(state_local, decay_local, span_count, 1)
    attended = attended_local + jnp.einsum("thc,hcd->thd", carried, state_in, precision=highest)

    def value_head(attended_in, weight_in):
        normed = attended_in * lax.rsqrt(
            jnp.mean(attended_in * attended_in, axis=-1, keepdims=True) + epsilon
        )
        return jnp.einsum("thd,hd->t", normed, weight_in, precision=highest)

    partial_value, pull_value = jax.vjp(value_head, attended, value_weight.reshape(head_count, DV))
    value_pred = butterfly_sum(partial_value, "head")
    residual = value_pred - targets[0]
    grad_attended, grad_weight = pull_value(residual)
    grad_carried = jnp.einsum("thd,hcd->thc", grad_attended, state_in, precision=highest)
    grad_direct = jnp.einsum("thc,thd->hcd", carried, grad_attended, precision=highest)
    inner_grads = pull_inner((grad_attended, grad_carried))

    grad_state = gather_scan(grad_direct, decay_local, span_count, -1)
    grad_decay = jnp.sum(state_in * grad_state, axis=-1)
    summary_grads = pull_summary((grad_state, grad_decay))

    grad_query = inner_grads[0]
    grad_key = inner_grads[1] + summary_grads[0]
    grad_value = inner_grads[2] + summary_grads[1]
    grad_logit = inner_grads[3] + summary_grads[2]
    grad_bias = inner_grads[4] + summary_grads[3]
    token_total = token_count * lax.axis_size("ctx") * lax.axis_size("rep")
    both_total = butterfly_sum(
        butterfly_sum(jnp.concatenate([grad_bias.reshape(-1), grad_weight.reshape(-1)]), "rep"),
        "ctx",
    )
    bias_total, weight_total = jnp.split(both_total, 2)

    def to_rows(array):
        return array.reshape(1, token_count, -1).astype(jnp.bfloat16)

    return (
        value_pred[None],
        to_rows(grad_query),
        to_rows(grad_key),
        to_rows(grad_value),
        to_rows(grad_logit),
        bias_total / token_total,
        weight_total / token_total,
    )


def solution(mesh):
    in_specs = (
        P(("groups", "rep"), "ctx", "head"),
        P(("groups", "rep"), "ctx", "head"),
        P(("groups", "rep"), "ctx", "head"),
        P(("groups", "rep"), "ctx", "head"),
        P("head"),
        P("head"),
        P(("groups", "rep"), "ctx"),
        P(("groups", "rep"), "ctx"),
        P(("groups", "rep"), "ctx"),
    )
    out_specs = (
        P(("groups", "rep"), "ctx"),
        P(("groups", "rep"), "ctx", "head"),
        P(("groups", "rep"), "ctx", "head"),
        P(("groups", "rep"), "ctx", "head"),
        P(("groups", "rep"), "ctx", "head"),
        P(("groups", "head")),
        P(("groups", "head")),
    )
    return jax.shard_map(
        on_device, mesh=mesh, in_specs=in_specs, out_specs=out_specs, check_vma=False
    )
```

```python
import jax
import jax.numpy as jnp
from jax import lax
from jax.sharding import PartitionSpec as P

DK = 128
DV = 128


epsilon = 1.0
gate_scale = 16.0
highest = lax.Precision.HIGHEST


def from_behind(value, axis, by):
    length = lax.axis_size(axis)
    pairs = [(i, i + by) for i in range(length) if 0 <= i + by < length]
    return lax.ppermute(value, axis, pairs)


def butterfly_sum(value, axis):
    length = lax.axis_size(axis)
    if length & (length - 1):
        return lax.psum(value, axis)
    bit = 1
    while bit < length:
        pairs = [(i, i ^ bit) for i in range(length)]
        value = value + lax.ppermute(value, axis, pairs)
        bit *= 2
    return value


def direct_sum(value, axis):
    length = lax.axis_size(axis)
    me = lax.axis_index(axis)
    terms = [value]
    for shift in range(1, length):
        pairs = [(i, (i + shift) % length) for i in range(length)]
        terms.append(lax.ppermute(value, axis, pairs))
    stacked = jnp.stack(terms)
    order = (me - jnp.arange(length, dtype=jnp.int32)) % length
    ordered = jnp.take(stacked, order, axis=0)
    total = ordered[0]
    for member in range(1, length):
        total = total + ordered[member]
    return total


def pack_state(state, factor):
    rows = jnp.zeros((state.shape[0], 8, state.shape[2]), state.dtype)
    rows = rows.at[:, 0, :].set(factor)
    return jnp.concatenate([state, rows], axis=1)


def gather_scan(state, factor, span_count, direction):
    channels = state.shape[1]
    near_a, near_b = None, None
    run_a, run_b = state, factor
    shift = 1
    while shift < span_count:
        last = 2 * shift >= span_count
        if last:
            far = from_behind(run_a, "ctx", direction * shift)
            far_a, far_b = far, None
        else:
            far = from_behind(pack_state(run_a, factor=run_b), "ctx", direction * shift)
            far_a, far_b = far[:, :channels], far[:, channels, :]
        if near_a is None:
            near_a, near_b = far_a, far_b
        else:
            near_a = far_a * near_b[..., None] + near_a
            near_b = None if last else far_b * near_b
        if not last:
            run_a = far_a * run_b[..., None] + run_a
            run_b = far_b * run_b
        shift *= 2
    if near_a is None:
        return jnp.zeros_like(state)
    return near_a


def log_decay(logit_in, bias_in):
    return jax.nn.log_sigmoid(logit_in + bias_in) / gate_scale


def segment_ids(start_flags):
    return jnp.cumsum(start_flags, axis=0, dtype=jnp.int32)


def block_inner(query_in, key_in, value_in, logit_in, bias_in, start_flags, kind_id):
    block_len = query_in.shape[0]
    channels = query_in.shape[2]
    log_cum = jnp.cumsum(log_decay(logit_in, bias_in), axis=0)
    segment = segment_ids(start_flags)
    alive_mask = (segment == 0).astype(jnp.float32)
    offsets = jnp.arange(block_len, dtype=jnp.int32)
    distance = offsets[:, None] - offsets[None, :]
    window = block_len // jnp.left_shift(jnp.ones_like(kind_id), kind_id)
    live_pairs = (
        (segment[:, None] == segment[None, :]) & (distance >= 0) & (distance < window)
    )
    query_dec = query_in * jnp.exp(log_cum) * channels ** (-0.5)
    key_dec = key_in * jnp.exp(-log_cum)
    scores = jnp.einsum("ihc,jhc->hij", query_dec, key_dec, precision=highest)
    block_probs = jnp.where(live_pairs[None], scores, 0.0).astype(jnp.bfloat16)
    inner_part = jnp.einsum(
        "hij,jhd->ihd",
        block_probs,
        value_in.astype(jnp.bfloat16),
        preferred_element_type=jnp.float32,
    )
    carried = query_dec * alive_mask[:, None, None]
    return inner_part, carried


def block_summary(key_in, value_in, logit_in, bias_in, start_flags):
    log_cum = jnp.cumsum(log_decay(logit_in, bias_in), axis=0)
    log_last = log_cum[-1]
    segment = segment_ids(start_flags)
    alive_last = (segment[-1] == 0).astype(jnp.float32)
    tail_mask = (segment == segment[-1]).astype(jnp.float32)
    key_tail = key_in * jnp.exp(log_last[None] - log_cum) * tail_mask[:, None, None]
    block_state = jnp.einsum("jhc,jhd->hcd", key_tail, value_in, precision=highest)
    block_decay = jnp.exp(log_last) * alive_last
    return block_state, block_decay


def on_device(
    queries,
    per_head_keys,
    value_rows,
    gate_logits,
    gate_bias,
    value_weight,
    targets,
    mask_ids,
    segment_starts,
):
    token_count = queries.shape[1]
    head_count = gate_bias.shape[0] // DK
    assert mask_ids.shape[1] == 1

    def to_heads(array):
        return array[0].reshape(token_count, head_count, -1).astype(jnp.float32)

    start_flags = segment_starts[0]
    kind_id = mask_ids[0, 0]
    query_f = to_heads(queries)
    key_f = to_heads(per_head_keys)
    value_f = to_heads(value_rows)
    logit_f = to_heads(gate_logits)
    bias_h = gate_bias.reshape(head_count, DK)

    def inner_terms(query_in, key_in, value_in, logit_in, bias_in):
        return block_inner(query_in, key_in, value_in, logit_in, bias_in, start_flags, kind_id)

    def summary_terms(key_in, value_in, logit_in, bias_in):
        return block_summary(key_in, value_in, logit_in, bias_in, start_flags)

    (attended_local, carried), pull_inner = jax.vjp(
        inner_terms, query_f, key_f, value_f, logit_f, bias_h
    )
    (state_local, decay_local), pull_summary = jax.vjp(
        summary_terms, key_f, value_f, logit_f, bias_h
    )

    span_count = lax.axis_size("ctx")
    state_in = gather_scan(state_local, decay_local, span_count, 1)
    attended = attended_local + jnp.einsum("thc,hcd->thd", carried, state_in, precision=highest)

    def value_head(attended_in, weight_in):
        normed = attended_in * lax.rsqrt(
            jnp.mean(attended_in * attended_in, axis=-1, keepdims=True) + epsilon
        )
        return jnp.einsum("thd,hd->t", normed, weight_in, precision=highest)

    partial_value, pull_value = jax.vjp(value_head, attended, value_weight.reshape(head_count, DV))
    value_pred = butterfly_sum(partial_value, "head")
    residual = value_pred - targets[0]
    grad_attended, grad_weight = pull_value(residual)
    grad_carried = jnp.einsum("thd,hcd->thc", grad_attended, state_in, precision=highest)
    grad_direct = jnp.einsum("thc,thd->hcd", carried, grad_attended, precision=highest)
    inner_grads = pull_inner((grad_attended, grad_carried))

    grad_state = gather_scan(grad_direct, decay_local, span_count, -1)
    grad_decay = jnp.sum(state_in * grad_state, axis=-1)
    summary_grads = pull_summary((grad_state, grad_decay))

    grad_query = inner_grads[0]
    grad_key = inner_grads[1] + summary_grads[0]
    grad_value = inner_grads[2] + summary_grads[1]
    grad_logit = inner_grads[3] + summary_grads[2]
    grad_bias = inner_grads[4] + summary_grads[3]
    token_total = token_count * lax.axis_size("ctx") * lax.axis_size("rep")
    both_total = direct_sum(
        butterfly_sum(jnp.concatenate([grad_bias.reshape(-1), grad_weight.reshape(-1)]), "rep"),
        "ctx",
    )
    bias_total, weight_total = jnp.split(both_total, 2)

    def to_rows(array):
        return array.reshape(1, token_count, -1).astype(jnp.bfloat16)

    return (
        value_pred[None],
        to_rows(grad_query),
        to_rows(grad_key),
        to_rows(grad_value),
        to_rows(grad_logit),
        bias_total / token_total,
        weight_total / token_total,
    )


def solution(mesh):
    in_specs = (
        P(("groups", "rep"), "ctx", "head"),
        P(("groups", "rep"), "ctx", "head"),
        P(("groups", "rep"), "ctx", "head"),
        P(("groups", "rep"), "ctx", "head"),
        P("head"),
        P("head"),
        P(("groups", "rep"), "ctx"),
        P(("groups", "rep"), "ctx"),
        P(("groups", "rep"), "ctx"),
    )
    out_specs = (
        P(("groups", "rep"), "ctx"),
        P(("groups", "rep"), "ctx", "head"),
        P(("groups", "rep"), "ctx", "head"),
        P(("groups", "rep"), "ctx", "head"),
        P(("groups", "rep"), "ctx", "head"),
        P(("groups", "head")),
        P(("groups", "head")),
    )
    return jax.shard_map(
        on_device, mesh=mesh, in_specs=in_specs, out_specs=out_specs, check_vma=False
    )
```

```python
import jax
import jax.numpy as jnp
from jax import lax
from jax.sharding import PartitionSpec as P

DK = 128
DV = 128


epsilon = 1.0
gate_scale = 16.0
highest = lax.Precision.HIGHEST


def from_behind(value, axis, by):
    length = lax.axis_size(axis)
    pairs = [(i, i + by) for i in range(length) if 0 <= i + by < length]
    return lax.ppermute(value, axis, pairs)


def butterfly_sum(value, axis):
    length = lax.axis_size(axis)
    if length & (length - 1):
        return lax.psum(value, axis)
    bit = 1
    while bit < length:
        pairs = [(i, i ^ bit) for i in range(length)]
        value = value + lax.ppermute(value, axis, pairs)
        bit *= 2
    return value


def direct_sum(value, axis):
    length = lax.axis_size(axis)
    me = lax.axis_index(axis)
    terms = [value]
    for shift in range(1, length):
        pairs = [(i, (i + shift) % length) for i in range(length)]
        terms.append(lax.ppermute(value, axis, pairs))
    stacked = jnp.stack(terms)
    order = (me - jnp.arange(length, dtype=jnp.int32)) % length
    ordered = jnp.take(stacked, order, axis=0)
    total = ordered[0]
    for member in range(1, length):
        total = total + ordered[member]
    return total


def pack_state(state, factor):
    rows = jnp.zeros((state.shape[0], 8, state.shape[2]), state.dtype)
    rows = rows.at[:, 0, :].set(factor)
    return jnp.concatenate([state, rows], axis=1)


def gather_scan(state, factor, span_count, direction):
    channels = state.shape[1]
    near_a, near_b = None, None
    run_a, run_b = state, factor
    shift = 1
    while shift < span_count:
        last = 2 * shift >= span_count
        if last:
            far = from_behind(run_a, "ctx", direction * shift)
            far_a, far_b = far, None
        else:
            far = from_behind(pack_state(run_a, factor=run_b), "ctx", direction * shift)
            far_a, far_b = far[:, :channels], far[:, channels, :]
        if near_a is None:
            near_a, near_b = far_a, far_b
        else:
            near_a = far_a * near_b[..., None] + near_a
            near_b = None if last else far_b * near_b
        if not last:
            run_a = far_a * run_b[..., None] + run_a
            run_b = far_b * run_b
        shift *= 2
    if near_a is None:
        return jnp.zeros_like(state)
    return near_a


def log_decay(logit_in, bias_in):
    return jax.nn.log_sigmoid(logit_in + bias_in) / gate_scale


def segment_ids(start_flags):
    return jnp.cumsum(start_flags, axis=0, dtype=jnp.int32)


def block_inner(query_in, key_in, value_in, logit_in, bias_in, start_flags, kind_id):
    block_len = query_in.shape[0]
    channels = query_in.shape[2]
    log_cum = jnp.cumsum(log_decay(logit_in, bias_in), axis=0)
    segment = segment_ids(start_flags)
    alive_mask = (segment == 0).astype(jnp.float32)
    offsets = jnp.arange(block_len, dtype=jnp.int32)
    distance = offsets[:, None] - offsets[None, :]
    window = block_len // jnp.left_shift(jnp.ones_like(kind_id), kind_id)
    live_pairs = (
        (segment[:, None] == segment[None, :]) & (distance >= 0) & (distance < window)
    )
    query_dec = query_in * jnp.exp(log_cum) * channels ** (-0.5)
    key_dec = key_in * jnp.exp(-log_cum)
    scores = jnp.einsum("ihc,jhc->hij", query_dec, key_dec, precision=highest)
    block_probs = jnp.where(live_pairs[None], scores, 0.0).astype(jnp.bfloat16)
    inner_part = jnp.einsum(
        "hij,jhd->ihd",
        block_probs,
        value_in.astype(jnp.bfloat16),
        preferred_element_type=jnp.float32,
    )
    carried = query_dec * alive_mask[:, None, None]
    return inner_part, carried


def block_summary(key_in, value_in, logit_in, bias_in, start_flags):
    log_cum = jnp.cumsum(log_decay(logit_in, bias_in), axis=0)
    log_last = log_cum[-1]
    segment = segment_ids(start_flags)
    alive_last = (segment[-1] == 0).astype(jnp.float32)
    tail_mask = (segment == segment[-1]).astype(jnp.float32)
    key_tail = key_in * jnp.exp(log_last[None] - log_cum) * tail_mask[:, None, None]
    block_state = jnp.einsum("jhc,jhd->hcd", key_tail, value_in, precision=highest)
    block_decay = jnp.exp(log_last) * alive_last
    return block_state, block_decay


def bias_transfer(key_in, value_in, logit_in, bias_in, start_flags, state_in, block_decay):
    slope = jax.nn.sigmoid(-(logit_in + bias_in)) / gate_scale
    log_cum = jnp.cumsum(log_decay(logit_in, bias_in), axis=0)
    log_last = log_cum[-1]
    segment = segment_ids(start_flags)
    tail_mask = (segment == segment[-1]).astype(jnp.float32)
    key_tail = key_in * jnp.exp(log_last[None] - log_cum) * tail_mask[:, None, None]
    from_end = jnp.cumsum(slope[::-1], axis=0)[::-1]
    later = jnp.concatenate([from_end[1:], jnp.zeros_like(from_end[:1])], axis=0)
    through = jnp.einsum("thc,thd->hcd", key_tail * later, value_in, precision=highest)
    return through + (block_decay * from_end[0])[..., None] * state_in


def on_device(
    queries,
    per_head_keys,
    value_rows,
    gate_logits,
    gate_bias,
    value_weight,
    targets,
    mask_ids,
    segment_starts,
):
    token_count = queries.shape[1]
    head_count = gate_bias.shape[0] // DK
    assert mask_ids.shape[1] == 1

    def to_heads(array):
        return array[0].reshape(token_count, head_count, -1).astype(jnp.float32)

    start_flags = segment_starts[0]
    kind_id = mask_ids[0, 0]
    query_f = to_heads(queries)
    key_f = to_heads(per_head_keys)
    value_f = to_heads(value_rows)
    logit_f = to_heads(gate_logits)
    bias_h = gate_bias.reshape(head_count, DK)

    def inner_terms(query_in, key_in, value_in, logit_in, bias_in):
        return block_inner(query_in, key_in, value_in, logit_in, bias_in, start_flags, kind_id)

    def summary_terms(key_in, value_in, logit_in, bias_in):
        return block_summary(key_in, value_in, logit_in, bias_in, start_flags)

    (attended_local, carried), pull_inner = jax.vjp(
        inner_terms, query_f, key_f, value_f, logit_f, bias_h
    )
    (state_local, decay_local), pull_summary = jax.vjp(
        summary_terms, key_f, value_f, logit_f, bias_h
    )

    span_count = lax.axis_size("ctx")
    state_in = gather_scan(state_local, decay_local, span_count, 1)
    attended = attended_local + jnp.einsum("thc,hcd->thd", carried, state_in, precision=highest)

    def value_head(attended_in, weight_in):
        normed = attended_in * lax.rsqrt(
            jnp.mean(attended_in * attended_in, axis=-1, keepdims=True) + epsilon
        )
        return jnp.einsum("thd,hd->t", normed, weight_in, precision=highest)

    partial_value, pull_value = jax.vjp(value_head, attended, value_weight.reshape(head_count, DV))
    value_pred = butterfly_sum(partial_value, "head")
    residual = value_pred - targets[0]
    grad_attended, grad_weight = pull_value(residual)
    grad_carried = jnp.einsum("thd,hcd->thc", grad_attended, state_in, precision=highest)
    grad_direct = jnp.einsum("thc,thd->hcd", carried, grad_attended, precision=highest)
    inner_grads = lax.optimization_barrier(pull_inner((grad_attended, grad_carried)))
    transfer = bias_transfer(key_f, value_f, logit_f, bias_h, start_flags, state_in, decay_local)
    transfer_in = gather_scan(transfer, decay_local, span_count, 1)
    bias_far = jnp.sum(grad_direct * transfer_in, axis=-1)

    grad_state = gather_scan(grad_direct, decay_local, span_count, -1)
    grad_decay = jnp.sum(state_in * grad_state, axis=-1)
    summary_grads = pull_summary((grad_state, grad_decay))

    grad_query = inner_grads[0]
    grad_key = inner_grads[1] + summary_grads[0]
    grad_value = inner_grads[2] + summary_grads[1]
    grad_logit = inner_grads[3] + summary_grads[2]
    grad_bias = inner_grads[4] + bias_far
    token_total = token_count * lax.axis_size("ctx") * lax.axis_size("rep")
    both_total = direct_sum(
        butterfly_sum(jnp.concatenate([grad_bias.reshape(-1), grad_weight.reshape(-1)]), "rep"),
        "ctx",
    )
    bias_total, weight_total = jnp.split(both_total, 2)

    def to_rows(array):
        return array.reshape(1, token_count, -1).astype(jnp.bfloat16)

    return (
        value_pred[None],
        to_rows(grad_query),
        to_rows(grad_key),
        to_rows(grad_value),
        to_rows(grad_logit),
        bias_total / token_total,
        weight_total / token_total,
    )


def solution(mesh):
    in_specs = (
        P(("groups", "rep"), "ctx", "head"),
        P(("groups", "rep"), "ctx", "head"),
        P(("groups", "rep"), "ctx", "head"),
        P(("groups", "rep"), "ctx", "head"),
        P("head"),
        P("head"),
        P(("groups", "rep"), "ctx"),
        P(("groups", "rep"), "ctx"),
        P(("groups", "rep"), "ctx"),
    )
    out_specs = (
        P(("groups", "rep"), "ctx"),
        P(("groups", "rep"), "ctx", "head"),
        P(("groups", "rep"), "ctx", "head"),
        P(("groups", "rep"), "ctx", "head"),
        P(("groups", "rep"), "ctx", "head"),
        P(("groups", "head")),
        P(("groups", "head")),
    )
    return jax.shard_map(
        on_device, mesh=mesh, in_specs=in_specs, out_specs=out_specs, check_vma=False
    )
```

```python
import jax
import jax.numpy as jnp
from jax import lax
from jax.sharding import PartitionSpec as P

DK = 128
DV = 128


epsilon = 1.0
gate_scale = 16.0
highest = lax.Precision.HIGH


def from_behind(value, axis, by):
    length = lax.axis_size(axis)
    pairs = [(i, i + by) for i in range(length) if 0 <= i + by < length]
    return lax.ppermute(value, axis, pairs)


def butterfly_sum(value, axis):
    length = lax.axis_size(axis)
    if length & (length - 1):
        return lax.psum(value, axis)
    bit = 1
    while bit < length:
        pairs = [(i, i ^ bit) for i in range(length)]
        value = value + lax.ppermute(value, axis, pairs)
        bit *= 2
    return value


def direct_sum(value, axis):
    length = lax.axis_size(axis)
    me = lax.axis_index(axis)
    terms = [value]
    for shift in range(1, length):
        pairs = [(i, (i + shift) % length) for i in range(length)]
        terms.append(lax.ppermute(value, axis, pairs))
    def from_member(member):
        source_shift = (me - member) % length
        picked = jnp.zeros_like(value)
        for shift, term in enumerate(terms):
            picked = jnp.where(source_shift == shift, term, picked)
        return picked

    total = from_member(0)
    for member in range(1, length):
        total = total + from_member(member)
    return total


def pack_state(state, factor):
    rows = jnp.zeros((state.shape[0], 8, state.shape[2]), state.dtype)
    rows = rows.at[:, 0, :].set(factor)
    return jnp.concatenate([state, rows], axis=1)


def gather_scan(state, factor, span_count, direction):
    channels = state.shape[1]
    near_a, near_b = None, None
    run_a, run_b = state, factor
    shift = 1
    while shift < span_count:
        last = 2 * shift >= span_count
        if last:
            far = from_behind(run_a, "ctx", direction * shift)
            far_a, far_b = far, None
        else:
            far = from_behind(pack_state(run_a, factor=run_b), "ctx", direction * shift)
            far_a, far_b = far[:, :channels], far[:, channels, :]
        if near_a is None:
            near_a, near_b = far_a, far_b
        else:
            near_a = far_a * near_b[..., None] + near_a
            near_b = None if last else far_b * near_b
        if not last:
            run_a = far_a * run_b[..., None] + run_a
            run_b = far_b * run_b
        shift *= 2
    if near_a is None:
        return jnp.zeros_like(state)
    return near_a


def log_decay(logit_in, bias_in):
    return jax.nn.log_sigmoid(logit_in + bias_in) / gate_scale


def segment_ids(start_flags):
    return jnp.cumsum(start_flags, axis=0, dtype=jnp.int32)


def block_inner(query_in, key_in, value_in, logit_in, bias_in, start_flags, kind_id):
    block_len = query_in.shape[0]
    channels = query_in.shape[2]
    log_cum = jnp.cumsum(log_decay(logit_in, bias_in), axis=0)
    segment = segment_ids(start_flags)
    alive_mask = (segment == 0).astype(jnp.float32)
    offsets = jnp.arange(block_len, dtype=jnp.int32)
    distance = offsets[:, None] - offsets[None, :]
    window = block_len // jnp.left_shift(jnp.ones_like(kind_id), kind_id)
    live_pairs = (
        (segment[:, None] == segment[None, :]) & (distance >= 0) & (distance < window)
    )
    query_dec = query_in * jnp.exp(log_cum) * channels ** (-0.5)
    key_dec = key_in * jnp.exp(-log_cum)
    scores = jnp.einsum("ihc,jhc->hij", query_dec, key_dec, precision=highest)
    block_probs = jnp.where(live_pairs[None], scores, 0.0).astype(jnp.bfloat16)
    inner_part = jnp.einsum(
        "hij,jhd->ihd",
        block_probs,
        value_in.astype(jnp.bfloat16),
        preferred_element_type=jnp.float32,
    )
    carried = query_dec * alive_mask[:, None, None]
    return inner_part, carried


def block_summary(key_in, value_in, logit_in, bias_in, start_flags):
    log_cum = jnp.cumsum(log_decay(logit_in, bias_in), axis=0)
    log_last = log_cum[-1]
    segment = segment_ids(start_flags)
    alive_last = (segment[-1] == 0).astype(jnp.float32)
    tail_mask = (segment == segment[-1]).astype(jnp.float32)
    key_tail = key_in * jnp.exp(log_last[None] - log_cum) * tail_mask[:, None, None]
    block_state = jnp.einsum("jhc,jhd->hcd", key_tail, value_in, precision=highest)
    block_decay = jnp.exp(log_last) * alive_last
    return block_state, block_decay


def on_device(
    queries,
    per_head_keys,
    value_rows,
    gate_logits,
    gate_bias,
    value_weight,
    targets,
    mask_ids,
    segment_starts,
):
    token_count = queries.shape[1]
    head_count = gate_bias.shape[0] // DK
    assert mask_ids.shape[1] == 1

    def to_heads(array):
        return array[0].reshape(token_count, head_count, -1).astype(jnp.float32)

    start_flags = segment_starts[0]
    kind_id = mask_ids[0, 0]
    query_f = to_heads(queries)
    key_f = to_heads(per_head_keys)
    value_f = to_heads(value_rows)
    logit_f = to_heads(gate_logits)
    bias_h = gate_bias.reshape(head_count, DK)

    def inner_terms(query_in, key_in, value_in, logit_in, bias_in):
        return block_inner(query_in, key_in, value_in, logit_in, bias_in, start_flags, kind_id)

    def summary_terms(key_in, value_in, logit_in, bias_in):
        return block_summary(key_in, value_in, logit_in, bias_in, start_flags)

    (attended_local, carried), pull_inner = jax.vjp(
        inner_terms, query_f, key_f, value_f, logit_f, bias_h
    )
    (state_local, decay_local), pull_summary = jax.vjp(
        summary_terms, key_f, value_f, logit_f, bias_h
    )

    span_count = lax.axis_size("ctx")
    state_in = gather_scan(state_local, decay_local, span_count, 1)
    attended = attended_local + jnp.einsum("thc,hcd->thd", carried, state_in, precision=highest)

    def value_head(attended_in, weight_in):
        normed = attended_in * lax.rsqrt(
            jnp.mean(attended_in * attended_in, axis=-1, keepdims=True) + epsilon
        )
        return jnp.einsum("thd,hd->t", normed, weight_in, precision=highest)

    partial_value, pull_value = jax.vjp(value_head, attended, value_weight.reshape(head_count, DV))
    value_pred = butterfly_sum(partial_value, "head")
    residual = value_pred - targets[0]
    grad_attended, grad_weight = pull_value(residual)
    grad_carried = jnp.einsum("thd,hcd->thc", grad_attended, state_in, precision=highest)
    grad_direct = jnp.einsum("thc,thd->hcd", carried, grad_attended, precision=highest)
    inner_grads = pull_inner((grad_attended, grad_carried))

    grad_state = gather_scan(grad_direct, decay_local, span_count, -1)
    grad_decay = jnp.sum(state_in * grad_state, axis=-1)
    summary_grads = pull_summary((grad_state, grad_decay))

    grad_query = inner_grads[0]
    grad_key = inner_grads[1] + summary_grads[0]
    grad_value = inner_grads[2] + summary_grads[1]
    grad_logit = inner_grads[3] + summary_grads[2]
    grad_bias = inner_grads[4] + summary_grads[3]
    token_total = token_count * lax.axis_size("ctx") * lax.axis_size("rep")
    both_total = direct_sum(
        butterfly_sum(jnp.concatenate([grad_bias.reshape(-1), grad_weight.reshape(-1)]), "rep"),
        "ctx",
    )
    bias_total, weight_total = jnp.split(both_total, 2)

    def to_rows(array):
        return array.reshape(1, token_count, -1).astype(jnp.bfloat16)

    return (
        value_pred[None],
        to_rows(grad_query),
        to_rows(grad_key),
        to_rows(grad_value),
        to_rows(grad_logit),
        bias_total / token_total,
        weight_total / token_total,
    )


def solution(mesh):
    in_specs = (
        P(("groups", "rep"), "ctx", "head"),
        P(("groups", "rep"), "ctx", "head"),
        P(("groups", "rep"), "ctx", "head"),
        P(("groups", "rep"), "ctx", "head"),
        P("head"),
        P("head"),
        P(("groups", "rep"), "ctx"),
        P(("groups", "rep"), "ctx"),
        P(("groups", "rep"), "ctx"),
    )
    out_specs = (
        P(("groups", "rep"), "ctx"),
        P(("groups", "rep"), "ctx", "head"),
        P(("groups", "rep"), "ctx", "head"),
        P(("groups", "rep"), "ctx", "head"),
        P(("groups", "rep"), "ctx", "head"),
        P(("groups", "head")),
        P(("groups", "head")),
    )
    return jax.shard_map(
        on_device, mesh=mesh, in_specs=in_specs, out_specs=out_specs, check_vma=False
    )
```

```python
import jax
import jax.numpy as jnp
from jax import lax
from jax.sharding import PartitionSpec as P

DK = 128
DV = 128


epsilon = 1.0
gate_scale = 16.0
highest = lax.Precision.HIGH


def from_behind(value, axis, by):
    length = lax.axis_size(axis)
    pairs = [(i, i + by) for i in range(length) if 0 <= i + by < length]
    return lax.ppermute(value, axis, pairs)


def butterfly_sum(value, axis):
    length = lax.axis_size(axis)
    if length & (length - 1):
        return lax.psum(value, axis)
    bit = 1
    while bit < length:
        pairs = [(i, i ^ bit) for i in range(length)]
        value = value + lax.ppermute(value, axis, pairs)
        bit *= 2
    return value


def direct_sum(value, axis):
    length = lax.axis_size(axis)
    me = lax.axis_index(axis)
    terms = [value]
    for shift in range(1, length):
        pairs = [(i, (i + shift) % length) for i in range(length)]
        terms.append(lax.ppermute(value, axis, pairs))
    def from_member(member):
        source_shift = (me - member) % length
        picked = jnp.zeros_like(value)
        for shift, term in enumerate(terms):
            picked = jnp.where(source_shift == shift, term, picked)
        return picked

    total = from_member(0)
    for member in range(1, length):
        total = total + from_member(member)
    return total


def pack_state(state, factor):
    rows = jnp.zeros((state.shape[0], 8, state.shape[2]), state.dtype)
    rows = rows.at[:, 0, :].set(factor)
    return jnp.concatenate([state, rows], axis=1)


def gather_scan(state, factor, span_count, direction):
    channels = state.shape[1]
    near_a, near_b = None, None
    run_a, run_b = state, factor
    shift = 1
    while shift < span_count:
        last = 2 * shift >= span_count
        if last:
            far = from_behind(run_a, "ctx", direction * shift)
            far_a, far_b = far, None
        else:
            far = from_behind(pack_state(run_a, factor=run_b), "ctx", direction * shift)
            far_a, far_b = far[:, :channels], far[:, channels, :]
        if near_a is None:
            near_a, near_b = far_a, far_b
        else:
            near_a = far_a * near_b[..., None] + near_a
            near_b = None if last else far_b * near_b
        if not last:
            run_a = far_a * run_b[..., None] + run_a
            run_b = far_b * run_b
        shift *= 2
    if near_a is None:
        return jnp.zeros_like(state)
    return near_a


def log_decay(logit_in, bias_in):
    return jax.nn.log_sigmoid(logit_in + bias_in) / gate_scale


def segment_ids(start_flags):
    return jnp.cumsum(start_flags, axis=0, dtype=jnp.int32)


def block_inner(query_in, key_in, value_in, logit_in, bias_in, start_flags, kind_id):
    block_len = query_in.shape[0]
    channels = query_in.shape[2]
    log_cum = jnp.cumsum(log_decay(logit_in, bias_in), axis=0)
    segment = segment_ids(start_flags)
    alive_mask = (segment == 0).astype(jnp.float32)
    offsets = jnp.arange(block_len, dtype=jnp.int32)
    distance = offsets[:, None] - offsets[None, :]
    window = block_len // jnp.left_shift(jnp.ones_like(kind_id), kind_id)
    live_pairs = (
        (segment[:, None] == segment[None, :]) & (distance >= 0) & (distance < window)
    )
    query_dec = query_in * jnp.exp(log_cum) * channels ** (-0.5)
    key_dec = key_in * jnp.exp(-log_cum)
    scores = jnp.einsum("ihc,jhc->hij", query_dec, key_dec, precision=highest)
    block_probs = jnp.where(live_pairs[None], scores, 0.0).astype(jnp.bfloat16)
    inner_part = jnp.einsum(
        "hij,jhd->ihd",
        block_probs,
        value_in.astype(jnp.bfloat16),
        preferred_element_type=jnp.float32,
    )
    carried = query_dec * alive_mask[:, None, None]
    return inner_part, carried


def block_summary(key_in, value_in, logit_in, bias_in, start_flags):
    log_cum = jnp.cumsum(log_decay(logit_in, bias_in), axis=0)
    log_last = log_cum[-1]
    segment = segment_ids(start_flags)
    last_segment = jnp.sum(start_flags)
    alive_last = (last_segment == 0).astype(jnp.float32)
    tail_mask = (segment == last_segment).astype(jnp.float32)
    key_tail = key_in * jnp.exp(log_last[None] - log_cum) * tail_mask[:, None, None]
    block_state = jnp.einsum("jhc,jhd->hcd", key_tail, value_in, precision=highest)
    block_decay = jnp.exp(log_last) * alive_last
    return block_state, block_decay


def on_device(
    queries,
    per_head_keys,
    value_rows,
    gate_logits,
    gate_bias,
    value_weight,
    targets,
    mask_ids,
    segment_starts,
):
    token_count = queries.shape[1]
    head_count = gate_bias.shape[0] // DK
    assert mask_ids.shape[1] == 1

    def to_heads(array):
        return array[0].reshape(token_count, head_count, -1).astype(jnp.float32)

    start_flags = segment_starts[0]
    kind_id = mask_ids[0, 0]
    query_f = to_heads(queries)
    key_f = to_heads(per_head_keys)
    value_f = to_heads(value_rows)
    logit_f = to_heads(gate_logits)
    bias_h = gate_bias.reshape(head_count, DK)

    def inner_terms(query_in, key_in, value_in, logit_in, bias_in):
        return block_inner(query_in, key_in, value_in, logit_in, bias_in, start_flags, kind_id)

    def summary_terms(key_in, value_in, logit_in, bias_in):
        return block_summary(key_in, value_in, logit_in, bias_in, start_flags)

    (attended_local, carried), pull_inner = jax.vjp(
        inner_terms, query_f, key_f, value_f, logit_f, bias_h
    )
    (state_local, decay_local), pull_summary = jax.vjp(
        summary_terms, key_f, value_f, logit_f, bias_h
    )

    span_count = lax.axis_size("ctx")
    state_in = gather_scan(state_local, decay_local, span_count, 1)
    attended = attended_local + jnp.einsum("thc,hcd->thd", carried, state_in, precision=highest)

    def value_head(attended_in, weight_in):
        normed = attended_in * lax.rsqrt(
            jnp.mean(attended_in * attended_in, axis=-1, keepdims=True) + epsilon
        )
        return jnp.einsum("thd,hd->t", normed, weight_in, precision=highest)

    partial_value, pull_value = jax.vjp(value_head, attended, value_weight.reshape(head_count, DV))
    unit_attended = pull_value(jnp.ones_like(partial_value))[0]
    value_pred = butterfly_sum(partial_value, "head")
    residual = value_pred - targets[0]
    grad_attended = unit_attended * residual[:, None, None]
    grad_weight = pull_value(residual)[1]
    grad_carried = jnp.einsum("thd,hcd->thc", grad_attended, state_in, precision=highest)
    grad_direct = jnp.einsum("thc,thd->hcd", carried, grad_attended, precision=highest)
    inner_grads = pull_inner((grad_attended, grad_carried))

    grad_state = gather_scan(grad_direct, decay_local, span_count, -1)
    grad_decay = jnp.sum(state_in * grad_state, axis=-1)
    summary_grads = pull_summary((grad_state, grad_decay))

    grad_query = inner_grads[0]
    grad_key = inner_grads[1] + summary_grads[0]
    grad_value = inner_grads[2] + summary_grads[1]
    grad_logit = inner_grads[3] + summary_grads[2]
    grad_bias = inner_grads[4] + summary_grads[3]
    token_total = token_count * lax.axis_size("ctx") * lax.axis_size("rep")
    both_total = direct_sum(
        butterfly_sum(jnp.concatenate([grad_bias.reshape(-1), grad_weight.reshape(-1)]), "rep"),
        "ctx",
    )
    bias_total, weight_total = jnp.split(both_total, 2)

    def to_rows(array):
        return array.reshape(1, token_count, -1).astype(jnp.bfloat16)

    return (
        value_pred[None],
        to_rows(grad_query),
        to_rows(grad_key),
        to_rows(grad_value),
        to_rows(grad_logit),
        bias_total / token_total,
        weight_total / token_total,
    )


def solution(mesh):
    in_specs = (
        P(("groups", "rep"), "ctx", "head"),
        P(("groups", "rep"), "ctx", "head"),
        P(("groups", "rep"), "ctx", "head"),
        P(("groups", "rep"), "ctx", "head"),
        P("head"),
        P("head"),
        P(("groups", "rep"), "ctx"),
        P(("groups", "rep"), "ctx"),
        P(("groups", "rep"), "ctx"),
    )
    out_specs = (
        P(("groups", "rep"), "ctx"),
        P(("groups", "rep"), "ctx", "head"),
        P(("groups", "rep"), "ctx", "head"),
        P(("groups", "rep"), "ctx", "head"),
        P(("groups", "rep"), "ctx", "head"),
        P(("groups", "head")),
        P(("groups", "head")),
    )
    return jax.shard_map(
        on_device, mesh=mesh, in_specs=in_specs, out_specs=out_specs, check_vma=False
    )
```

```python
import jax
import jax.numpy as jnp
from jax import lax
from jax.sharding import PartitionSpec as P

DK = 128
DV = 128


epsilon = 1.0
gate_scale = 16.0
highest = lax.Precision.HIGH


def from_behind(value, axis, by):
    length = lax.axis_size(axis)
    pairs = [(i, i + by) for i in range(length) if 0 <= i + by < length]
    return lax.ppermute(value, axis, pairs)


def butterfly_sum(value, axis):
    length = lax.axis_size(axis)
    if length & (length - 1):
        return lax.psum(value, axis)
    bit = 1
    while bit < length:
        pairs = [(i, i ^ bit) for i in range(length)]
        value = value + lax.ppermute(value, axis, pairs)
        bit *= 2
    return value


def direct_sum(value, axis):
    length = lax.axis_size(axis)
    me = lax.axis_index(axis)
    terms = [value]
    for shift in range(1, length):
        pairs = [(i, (i + shift) % length) for i in range(length)]
        terms.append(lax.ppermute(value, axis, pairs))
    def from_member(member):
        source_shift = (me - member) % length
        picked = jnp.zeros_like(value)
        for shift, term in enumerate(terms):
            picked = jnp.where(source_shift == shift, term, picked)
        return picked

    total = from_member(0)
    for member in range(1, length):
        total = total + from_member(member)
    return total


def pack_state(state, factor):
    rows = jnp.zeros((state.shape[0], 8, state.shape[2]), state.dtype)
    rows = rows.at[:, 0, :].set(factor)
    return jnp.concatenate([state, rows], axis=1)


def gather_scan(state, factor, span_count, direction):
    channels = state.shape[1]
    near_a, near_b = None, None
    run_a, run_b = state, factor
    shift = 1
    while shift < span_count:
        last = 2 * shift >= span_count
        if last:
            far = from_behind(run_a, "ctx", direction * shift)
            far_a, far_b = far, None
        else:
            far = from_behind(pack_state(run_a, factor=run_b), "ctx", direction * shift)
            far_a, far_b = far[:, :channels], far[:, channels, :]
        if near_a is None:
            near_a, near_b = far_a, far_b
        else:
            near_a = far_a * near_b[..., None] + near_a
            near_b = None if last else far_b * near_b
        if not last:
            run_a = far_a * run_b[..., None] + run_a
            run_b = far_b * run_b
        shift *= 2
    if near_a is None:
        return jnp.zeros_like(state)
    return near_a


def log_decay(logit_in, bias_in):
    return jax.nn.log_sigmoid(logit_in + bias_in) / gate_scale


def segment_ids(start_flags):
    return jnp.cumsum(start_flags, axis=0, dtype=jnp.int32)


def block_inner(query_in, key_in, value_in, logit_in, bias_in, start_flags, kind_id):
    block_len = query_in.shape[0]
    channels = query_in.shape[2]
    log_cum = jnp.cumsum(log_decay(logit_in, bias_in), axis=0)
    segment = segment_ids(start_flags)
    alive_mask = (segment == 0).astype(jnp.float32)
    offsets = jnp.arange(block_len, dtype=jnp.int32)
    distance = offsets[:, None] - offsets[None, :]
    window = block_len // jnp.left_shift(jnp.ones_like(kind_id), kind_id)
    live_pairs = (
        (segment[:, None] == segment[None, :]) & (distance >= 0) & (distance < window)
    )
    query_dec = query_in * jnp.exp(log_cum) * channels ** (-0.5)
    key_dec = key_in * jnp.exp(-log_cum)
    scores = jnp.einsum("ihc,jhc->hij", query_dec, key_dec, precision=highest)
    block_probs = jnp.where(live_pairs[None], scores, 0.0).astype(jnp.bfloat16)
    inner_part = jnp.einsum(
        "hij,jhd->ihd",
        block_probs,
        value_in.astype(jnp.bfloat16),
        preferred_element_type=jnp.float32,
    )
    carried = query_dec * alive_mask[:, None, None]
    return inner_part, carried


def block_summary(key_in, value_in, logit_in, bias_in, start_flags):
    log_cum = jnp.cumsum(log_decay(logit_in, bias_in), axis=0)
    log_last = log_cum[-1]
    segment = segment_ids(start_flags)
    alive_last = (segment[-1] == 0).astype(jnp.float32)
    tail_mask = (segment == segment[-1]).astype(jnp.float32)
    key_tail = key_in * jnp.exp(log_last[None] - log_cum) * tail_mask[:, None, None]
    block_state = jnp.einsum("jhc,jhd->hcd", key_tail, value_in, precision=highest)
    block_decay = jnp.exp(log_last) * alive_last
    return block_state, block_decay


def bias_transfer(key_in, value_in, logit_in, bias_in, start_flags, state_in, block_decay):
    slope = jax.nn.sigmoid(-(logit_in + bias_in)) / gate_scale
    log_cum = jnp.cumsum(log_decay(logit_in, bias_in), axis=0)
    log_last = log_cum[-1]
    segment = segment_ids(start_flags)
    tail_mask = (segment == segment[-1]).astype(jnp.float32)
    key_tail = key_in * jnp.exp(log_last[None] - log_cum) * tail_mask[:, None, None]
    from_end = jnp.cumsum(slope[::-1], axis=0)[::-1]
    later = jnp.concatenate([from_end[1:], jnp.zeros_like(from_end[:1])], axis=0)
    through = jnp.einsum("thc,thd->hcd", key_tail * later, value_in, precision=highest)
    return through + (block_decay * from_end[0])[..., None] * state_in


def on_device(
    queries,
    per_head_keys,
    value_rows,
    gate_logits,
    gate_bias,
    value_weight,
    targets,
    mask_ids,
    segment_starts,
):
    token_count = queries.shape[1]
    head_count = gate_bias.shape[0] // DK
    assert mask_ids.shape[1] == 1

    def to_heads(array):
        return array[0].reshape(token_count, head_count, -1).astype(jnp.float32)

    start_flags = segment_starts[0]
    kind_id = mask_ids[0, 0]
    query_f = to_heads(queries)
    key_f = to_heads(per_head_keys)
    value_f = to_heads(value_rows)
    logit_f = to_heads(gate_logits)
    bias_h = gate_bias.reshape(head_count, DK)

    def inner_terms(query_in, key_in, value_in, logit_in, bias_in):
        return block_inner(query_in, key_in, value_in, logit_in, bias_in, start_flags, kind_id)

    def summary_terms(key_in, value_in, logit_in, bias_in):
        return block_summary(key_in, value_in, logit_in, bias_in, start_flags)

    (attended_local, carried), pull_inner = jax.vjp(
        inner_terms, query_f, key_f, value_f, logit_f, bias_h
    )
    (state_local, decay_local), pull_summary = jax.vjp(
        summary_terms, key_f, value_f, logit_f, bias_h
    )

    span_count = lax.axis_size("ctx")
    state_in = gather_scan(state_local, decay_local, span_count, 1)
    attended = attended_local + jnp.einsum("thc,hcd->thd", carried, state_in, precision=highest)

    def value_head(attended_in, weight_in):
        normed = attended_in * lax.rsqrt(
            jnp.mean(attended_in * attended_in, axis=-1, keepdims=True) + epsilon
        )
        return jnp.einsum("thd,hd->t", normed, weight_in, precision=highest)

    partial_value, pull_value = jax.vjp(value_head, attended, value_weight.reshape(head_count, DV))
    value_pred = butterfly_sum(partial_value, "head")
    residual = value_pred - targets[0]
    grad_attended, grad_weight = pull_value(residual)
    grad_carried = jnp.einsum("thd,hcd->thc", grad_attended, state_in, precision=highest)
    grad_direct = jnp.einsum("thc,thd->hcd", carried, grad_attended, precision=highest)
    inner_grads = pull_inner((grad_attended, grad_carried))
    transfer = bias_transfer(key_f, value_f, logit_f, bias_h, start_flags, state_in, decay_local)

    grad_state = gather_scan(grad_direct, decay_local, span_count, -1)
    grad_decay = jnp.sum(state_in * grad_state, axis=-1)
    summary_grads = pull_summary((grad_state, grad_decay))

    grad_query = inner_grads[0]
    grad_key = inner_grads[1] + summary_grads[0]
    grad_value = inner_grads[2] + summary_grads[1]
    grad_logit = lax.optimization_barrier(inner_grads[3]) + summary_grads[2]
    grad_bias = inner_grads[4] + jnp.sum(grad_state * transfer, axis=-1)
    token_total = token_count * lax.axis_size("ctx") * lax.axis_size("rep")
    both_total = direct_sum(
        butterfly_sum(jnp.concatenate([grad_bias.reshape(-1), grad_weight.reshape(-1)]), "rep"),
        "ctx",
    )
    bias_total, weight_total = jnp.split(both_total, 2)

    def to_rows(array):
        return array.reshape(1, token_count, -1).astype(jnp.bfloat16)

    return (
        value_pred[None],
        to_rows(grad_query),
        to_rows(grad_key),
        to_rows(grad_value),
        to_rows(grad_logit),
        bias_total / token_total,
        weight_total / token_total,
    )


def solution(mesh):
    in_specs = (
        P(("groups", "rep"), "ctx", "head"),
        P(("groups", "rep"), "ctx", "head"),
        P(("groups", "rep"), "ctx", "head"),
        P(("groups", "rep"), "ctx", "head"),
        P("head"),
        P("head"),
        P(("groups", "rep"), "ctx"),
        P(("groups", "rep"), "ctx"),
        P(("groups", "rep"), "ctx"),
    )
    out_specs = (
        P(("groups", "rep"), "ctx"),
        P(("groups", "rep"), "ctx", "head"),
        P(("groups", "rep"), "ctx", "head"),
        P(("groups", "rep"), "ctx", "head"),
        P(("groups", "rep"), "ctx", "head"),
        P(("groups", "head")),
        P(("groups", "head")),
    )
    return jax.shard_map(
        on_device, mesh=mesh, in_specs=in_specs, out_specs=out_specs, check_vma=False
    )
```

```python
import jax
import jax.numpy as jnp
from jax import lax
from jax.sharding import PartitionSpec as P

DK = 128
DV = 128


epsilon = 1.0
gate_scale = 16.0
highest = lax.Precision.HIGH


def from_behind(value, axis, by):
    length = lax.axis_size(axis)
    pairs = [(i, i + by) for i in range(length) if 0 <= i + by < length]
    return lax.ppermute(value, axis, pairs)


def butterfly_sum(value, axis):
    length = lax.axis_size(axis)
    if length & (length - 1):
        return lax.psum(value, axis)
    bit = 1
    while bit < length:
        pairs = [(i, i ^ bit) for i in range(length)]
        value = value + lax.ppermute(value, axis, pairs)
        bit *= 2
    return value


def direct_sum(value, axis):
    length = lax.axis_size(axis)
    me = lax.axis_index(axis)
    terms = [value]
    for shift in range(1, length):
        pairs = [(i, (i + shift) % length) for i in range(length)]
        terms.append(lax.ppermute(value, axis, pairs))
    def from_member(member):
        source_shift = (me - member) % length
        picked = jnp.zeros_like(value)
        for shift, term in enumerate(terms):
            picked = jnp.where(source_shift == shift, term, picked)
        return picked

    total = from_member(0)
    for member in range(1, length):
        total = total + from_member(member)
    return total


def pack_state(state, factor):
    rows = jnp.zeros((state.shape[0], 8, state.shape[2]), state.dtype)
    rows = rows.at[:, 0, :].set(factor)
    return jnp.concatenate([state, rows], axis=1)


def gather_scan(state, factor, span_count, direction):
    channels = state.shape[1]
    near_a, near_b = None, None
    run_a, run_b = state, factor
    shift = 1
    while shift < span_count:
        last = 2 * shift >= span_count
        if last:
            far = from_behind(run_a, "ctx", direction * shift)
            far_a, far_b = far, None
        else:
            far = from_behind(pack_state(run_a, factor=run_b), "ctx", direction * shift)
            far_a, far_b = far[:, :channels], far[:, channels, :]
        if near_a is None:
            near_a, near_b = far_a, far_b
        else:
            near_a = far_a * near_b[..., None] + near_a
            near_b = None if last else far_b * near_b
        if not last:
            run_a = far_a * run_b[..., None] + run_a
            run_b = far_b * run_b
        shift *= 2
    if near_a is None:
        return jnp.zeros_like(state)
    return near_a


def log_decay(logit_in, bias_in):
    return jax.nn.log_sigmoid(logit_in + bias_in) / gate_scale


def segment_ids(start_flags):
    return jnp.cumsum(start_flags, axis=0, dtype=jnp.int32)


def block_inner(query_in, key_in, value_in, logit_in, bias_in, start_flags, kind_id):
    block_len = query_in.shape[0]
    channels = query_in.shape[2]
    log_cum = jnp.cumsum(log_decay(logit_in, bias_in), axis=0)
    segment = segment_ids(start_flags)
    alive_mask = (segment == 0).astype(jnp.float32)
    offsets = jnp.arange(block_len, dtype=jnp.int32)
    distance = offsets[:, None] - offsets[None, :]
    window = block_len // jnp.left_shift(jnp.ones_like(kind_id), kind_id)
    live_pairs = (
        (segment[:, None] == segment[None, :]) & (distance >= 0) & (distance < window)
    )
    query_dec = query_in * jnp.exp(log_cum) * channels ** (-0.5)
    key_dec = key_in * jnp.exp(-log_cum)
    scores = jnp.einsum("ihc,jhc->hij", query_dec, key_dec, precision=highest)
    block_probs = jnp.where(live_pairs[None], scores, 0.0).astype(jnp.bfloat16)
    inner_part = jnp.einsum(
        "hij,jhd->ihd",
        block_probs,
        value_in.astype(jnp.bfloat16),
        preferred_element_type=jnp.float32,
    )
    carried = query_dec * alive_mask[:, None, None]
    return inner_part, carried


def block_summary(key_in, value_in, logit_in, bias_in, start_flags):
    log_cum = jnp.cumsum(log_decay(logit_in, bias_in), axis=0)
    log_last = log_cum[-1]
    segment = segment_ids(start_flags)
    alive_last = (segment[-1] == 0).astype(jnp.float32)
    tail_mask = (segment == segment[-1]).astype(jnp.float32)
    key_tail = key_in * jnp.exp(log_last[None] - log_cum) * tail_mask[:, None, None]
    block_state = jnp.einsum("jhc,jhd->hcd", key_tail, value_in, precision=highest)
    block_decay = jnp.exp(log_last) * alive_last
    return block_state, block_decay


def on_device(
    queries,
    per_head_keys,
    value_rows,
    gate_logits,
    gate_bias,
    value_weight,
    targets,
    mask_ids,
    segment_starts,
):
    token_count = queries.shape[1]
    head_count = gate_bias.shape[0] // DK
    assert mask_ids.shape[1] == 1

    def to_heads(array):
        return array[0].reshape(token_count, head_count, -1).astype(jnp.float32)

    start_flags = segment_starts[0]
    kind_id = mask_ids[0, 0]
    rows_in = lax.optimization_barrier(
        jnp.concatenate([queries, per_head_keys, value_rows, gate_logits], axis=0)
    )
    query_f = to_heads(rows_in[0:1])
    key_f = to_heads(rows_in[1:2])
    value_f = to_heads(rows_in[2:3])
    logit_f = to_heads(rows_in[3:4])
    bias_h = gate_bias.reshape(head_count, DK)

    def inner_terms(query_in, key_in, value_in, logit_in, bias_in):
        return block_inner(query_in, key_in, value_in, logit_in, bias_in, start_flags, kind_id)

    def summary_terms(key_in, value_in, logit_in, bias_in):
        return block_summary(key_in, value_in, logit_in, bias_in, start_flags)

    (attended_local, carried), pull_inner = jax.vjp(
        inner_terms, query_f, key_f, value_f, logit_f, bias_h
    )
    (state_local, decay_local), pull_summary = jax.vjp(
        summary_terms, key_f, value_f, logit_f, bias_h
    )

    span_count = lax.axis_size("ctx")
    state_in = gather_scan(state_local, decay_local, span_count, 1)
    attended = attended_local + jnp.einsum("thc,hcd->thd", carried, state_in, precision=highest)

    def value_head(attended_in, weight_in):
        normed = attended_in * lax.rsqrt(
            jnp.mean(attended_in * attended_in, axis=-1, keepdims=True) + epsilon
        )
        return jnp.einsum("thd,hd->t", normed, weight_in, precision=highest)

    partial_value, pull_value = jax.vjp(value_head, attended, value_weight.reshape(head_count, DV))
    value_pred = butterfly_sum(partial_value, "head")
    residual = value_pred - targets[0]
    grad_attended, grad_weight = pull_value(residual)
    grad_carried = jnp.einsum("thd,hcd->thc", grad_attended, state_in, precision=highest)
    grad_direct = jnp.einsum("thc,thd->hcd", carried, grad_attended, precision=highest)
    inner_grads = pull_inner((grad_attended, grad_carried))

    grad_state = gather_scan(grad_direct, decay_local, span_count, -1)
    grad_decay = jnp.sum(state_in * grad_state, axis=-1)
    summary_grads = pull_summary((grad_state, grad_decay))

    grad_query = inner_grads[0]
    grad_key = inner_grads[1] + summary_grads[0]
    grad_value = inner_grads[2] + summary_grads[1]
    grad_logit = inner_grads[3] + summary_grads[2]
    grad_bias = inner_grads[4] + summary_grads[3]
    token_total = token_count * lax.axis_size("ctx") * lax.axis_size("rep")
    both_total = direct_sum(
        butterfly_sum(jnp.concatenate([grad_bias.reshape(-1), grad_weight.reshape(-1)]), "rep"),
        "ctx",
    )
    bias_total, weight_total = jnp.split(both_total, 2)

    def to_rows(array):
        return array.reshape(1, token_count, -1).astype(jnp.bfloat16)

    return (
        value_pred[None],
        to_rows(grad_query),
        to_rows(grad_key),
        to_rows(grad_value),
        to_rows(grad_logit),
        bias_total / token_total,
        weight_total / token_total,
    )


def solution(mesh):
    in_specs = (
        P(("groups", "rep"), "ctx", "head"),
        P(("groups", "rep"), "ctx", "head"),
        P(("groups", "rep"), "ctx", "head"),
        P(("groups", "rep"), "ctx", "head"),
        P("head"),
        P("head"),
        P(("groups", "rep"), "ctx"),
        P(("groups", "rep"), "ctx"),
        P(("groups", "rep"), "ctx"),
    )
    out_specs = (
        P(("groups", "rep"), "ctx"),
        P(("groups", "rep"), "ctx", "head"),
        P(("groups", "rep"), "ctx", "head"),
        P(("groups", "rep"), "ctx", "head"),
        P(("groups", "rep"), "ctx", "head"),
        P(("groups", "head")),
        P(("groups", "head")),
    )
    return jax.shard_map(
        on_device, mesh=mesh, in_specs=in_specs, out_specs=out_specs, check_vma=False
    )
```

```python
import jax
import jax.numpy as jnp
from jax import lax
from jax.sharding import PartitionSpec as P

DK = 128
DV = 128


epsilon = 1.0
gate_scale = 16.0
highest = lax.Precision.HIGH


def from_behind(value, axis, by):
    length = lax.axis_size(axis)
    pairs = [(i, i + by) for i in range(length) if 0 <= i + by < length]
    return lax.ppermute(value, axis, pairs)


def butterfly_sum(value, axis):
    length = lax.axis_size(axis)
    if length & (length - 1):
        return lax.psum(value, axis)
    bit = 1
    while bit < length:
        pairs = [(i, i ^ bit) for i in range(length)]
        value = value + lax.ppermute(value, axis, pairs)
        bit *= 2
    return value


def direct_sum(value, axis):
    length = lax.axis_size(axis)
    me = lax.axis_index(axis)
    terms = [value]
    for shift in range(1, length):
        pairs = [(i, (i + shift) % length) for i in range(length)]
        terms.append(lax.ppermute(value, axis, pairs))
    def from_member(member):
        source_shift = (me - member) % length
        picked = jnp.zeros_like(value)
        for shift, term in enumerate(terms):
            picked = jnp.where(source_shift == shift, term, picked)
        return picked

    total = from_member(0)
    for member in range(1, length):
        total = total + from_member(member)
    return total


def exchange_sum(value, axes):
    members = 1
    for axis in axes:
        members *= lax.axis_size(axis)
    tiled = jnp.broadcast_to(value[None], (members,) + value.shape)
    terms = lax.all_to_all(tiled, axes, 0, 0, tiled=True)
    total = terms[0]
    for member in range(1, members):
        total = total + terms[member]
    return total


def pack_state(state, factor):
    rows = jnp.zeros((state.shape[0], 8, state.shape[2]), state.dtype)
    rows = rows.at[:, 0, :].set(factor)
    return jnp.concatenate([state, rows], axis=1)


def gather_scan(state, factor, span_count, direction):
    channels = state.shape[1]
    near_a, near_b = None, None
    run_a, run_b = state, factor
    shift = 1
    while shift < span_count:
        last = 2 * shift >= span_count
        if last:
            far = from_behind(run_a, "ctx", direction * shift)
            far_a, far_b = far, None
        else:
            far = from_behind(pack_state(run_a, factor=run_b), "ctx", direction * shift)
            far_a, far_b = far[:, :channels], far[:, channels, :]
        if near_a is None:
            near_a, near_b = far_a, far_b
        else:
            near_a = far_a * near_b[..., None] + near_a
            near_b = None if last else far_b * near_b
        if not last:
            run_a = far_a * run_b[..., None] + run_a
            run_b = far_b * run_b
        shift *= 2
    if near_a is None:
        return jnp.zeros_like(state)
    return near_a


def log_decay(logit_in, bias_in):
    return jax.nn.log_sigmoid(logit_in + bias_in) / gate_scale


def segment_ids(start_flags):
    return jnp.cumsum(start_flags, axis=0, dtype=jnp.int32)


def block_inner(query_in, key_in, value_in, logit_in, bias_in, start_flags, kind_id):
    block_len = query_in.shape[0]
    channels = query_in.shape[2]
    log_cum = jnp.cumsum(log_decay(logit_in, bias_in), axis=0)
    segment = segment_ids(start_flags)
    alive_mask = (segment == 0).astype(jnp.float32)
    offsets = jnp.arange(block_len, dtype=jnp.int32)
    distance = offsets[:, None] - offsets[None, :]
    window = block_len // jnp.left_shift(jnp.ones_like(kind_id), kind_id)
    live_pairs = (
        (segment[:, None] == segment[None, :]) & (distance >= 0) & (distance < window)
    )
    query_dec = query_in * jnp.exp(log_cum) * channels ** (-0.5)
    key_dec = key_in * jnp.exp(-log_cum)
    scores = jnp.einsum("ihc,jhc->hij", query_dec, key_dec, precision=highest)
    block_probs = jnp.where(live_pairs[None], scores, 0.0).astype(jnp.bfloat16)
    inner_part = jnp.einsum(
        "hij,jhd->ihd",
        block_probs,
        value_in.astype(jnp.bfloat16),
        preferred_element_type=jnp.float32,
    )
    carried = query_dec * alive_mask[:, None, None]
    return inner_part, carried


def block_summary(key_in, value_in, logit_in, bias_in, start_flags):
    log_cum = jnp.cumsum(log_decay(logit_in, bias_in), axis=0)
    log_last = log_cum[-1]
    segment = segment_ids(start_flags)
    alive_last = (segment[-1] == 0).astype(jnp.float32)
    tail_mask = (segment == segment[-1]).astype(jnp.float32)
    key_tail = key_in * jnp.exp(log_last[None] - log_cum) * tail_mask[:, None, None]
    block_state = jnp.einsum("jhc,jhd->hcd", key_tail, value_in, precision=highest)
    block_decay = jnp.exp(log_last) * alive_last
    return block_state, block_decay


def on_device(
    queries,
    per_head_keys,
    value_rows,
    gate_logits,
    gate_bias,
    value_weight,
    targets,
    mask_ids,
    segment_starts,
):
    token_count = queries.shape[1]
    head_count = gate_bias.shape[0] // DK
    assert mask_ids.shape[1] == 1

    def to_heads(array):
        return array[0].reshape(token_count, head_count, -1).astype(jnp.float32)

    start_flags = segment_starts[0]
    kind_id = mask_ids[0, 0]
    rows_in = lax.optimization_barrier(
        jnp.concatenate([queries, per_head_keys, value_rows, gate_logits], axis=0)
    )
    query_f = to_heads(rows_in[0:1])
    key_f = to_heads(rows_in[1:2])
    value_f = to_heads(rows_in[2:3])
    logit_f = to_heads(rows_in[3:4])
    bias_h = gate_bias.reshape(head_count, DK)

    def inner_terms(query_in, key_in, value_in, logit_in, bias_in):
        return block_inner(query_in, key_in, value_in, logit_in, bias_in, start_flags, kind_id)

    def summary_terms(key_in, value_in, logit_in, bias_in):
        return block_summary(key_in, value_in, logit_in, bias_in, start_flags)

    (attended_local, carried), pull_inner = jax.vjp(
        inner_terms, query_f, key_f, value_f, logit_f, bias_h
    )
    (state_local, decay_local), pull_summary = jax.vjp(
        summary_terms, key_f, value_f, logit_f, bias_h
    )

    span_count = lax.axis_size("ctx")
    state_in = gather_scan(state_local, decay_local, span_count, 1)
    attended = attended_local + jnp.einsum("thc,hcd->thd", carried, state_in, precision=highest)

    def value_head(attended_in, weight_in):
        normed = attended_in * lax.rsqrt(
            jnp.mean(attended_in * attended_in, axis=-1, keepdims=True) + epsilon
        )
        return jnp.einsum("thd,hd->t", normed, weight_in, precision=highest)

    partial_value, pull_value = jax.vjp(value_head, attended, value_weight.reshape(head_count, DV))
    value_pred = butterfly_sum(partial_value, "head")
    residual = value_pred - targets[0]
    grad_attended, grad_weight = pull_value(residual)
    grad_carried = jnp.einsum("thd,hcd->thc", grad_attended, state_in, precision=highest)
    grad_direct = jnp.einsum("thc,thd->hcd", carried, grad_attended, precision=highest)
    inner_grads = pull_inner((grad_attended, grad_carried))

    grad_state = gather_scan(grad_direct, decay_local, span_count, -1)
    grad_decay = jnp.sum(state_in * grad_state, axis=-1)
    summary_grads = pull_summary((grad_state, grad_decay))

    grad_query = inner_grads[0]
    grad_key = inner_grads[1] + summary_grads[0]
    grad_value = inner_grads[2] + summary_grads[1]
    grad_logit = inner_grads[3] + summary_grads[2]
    grad_bias = inner_grads[4] + summary_grads[3]
    token_total = token_count * lax.axis_size("ctx") * lax.axis_size("rep")
    both_total = exchange_sum(
        jnp.concatenate([grad_bias.reshape(-1), grad_weight.reshape(-1)]), ("ctx", "rep")
    )
    bias_total, weight_total = jnp.split(both_total, 2)

    def to_rows(array):
        return array.reshape(1, token_count, -1).astype(jnp.bfloat16)

    return (
        value_pred[None],
        to_rows(grad_query),
        to_rows(grad_key),
        to_rows(grad_value),
        to_rows(grad_logit),
        bias_total / token_total,
        weight_total / token_total,
    )


def solution(mesh):
    in_specs = (
        P(("groups", "rep"), "ctx", "head"),
        P(("groups", "rep"), "ctx", "head"),
        P(("groups", "rep"), "ctx", "head"),
        P(("groups", "rep"), "ctx", "head"),
        P("head"),
        P("head"),
        P(("groups", "rep"), "ctx"),
        P(("groups", "rep"), "ctx"),
        P(("groups", "rep"), "ctx"),
    )
    out_specs = (
        P(("groups", "rep"), "ctx"),
        P(("groups", "rep"), "ctx", "head"),
        P(("groups", "rep"), "ctx", "head"),
        P(("groups", "rep"), "ctx", "head"),
        P(("groups", "rep"), "ctx", "head"),
        P(("groups", "head")),
        P(("groups", "head")),
    )
    return jax.shard_map(
        on_device, mesh=mesh, in_specs=in_specs, out_specs=out_specs, check_vma=False
    )
```

```python
import jax
import jax.numpy as jnp
from jax import lax
from jax.sharding import PartitionSpec as P

DK = 128
DV = 128


epsilon = 1.0
gate_scale = 16.0
highest = lax.Precision.HIGH


def from_behind(value, axis, by):
    length = lax.axis_size(axis)
    pairs = [(i, i + by) for i in range(length) if 0 <= i + by < length]
    return lax.ppermute(value, axis, pairs)


def butterfly_sum(value, axis):
    length = lax.axis_size(axis)
    if length & (length - 1):
        return lax.psum(value, axis)
    bit = 1
    while bit < length:
        pairs = [(i, i ^ bit) for i in range(length)]
        value = value + lax.ppermute(value, axis, pairs)
        bit *= 2
    return value


def direct_sum(value, axis):
    length = lax.axis_size(axis)
    me = lax.axis_index(axis)
    terms = [value]
    for shift in range(1, length):
        pairs = [(i, (i + shift) % length) for i in range(length)]
        terms.append(lax.ppermute(value, axis, pairs))
    def from_member(member):
        source_shift = (me - member) % length
        picked = jnp.zeros_like(value)
        for shift, term in enumerate(terms):
            picked = jnp.where(source_shift == shift, term, picked)
        return picked

    total = from_member(0)
    for member in range(1, length):
        total = total + from_member(member)
    return total


def pack_state(state, factor):
    rows = jnp.zeros((state.shape[0], 8, state.shape[2]), state.dtype)
    rows = rows.at[:, 0, :].set(factor)
    return jnp.concatenate([state, rows], axis=1)


def gather_scan(state, factor, span_count, direction):
    channels = state.shape[1]
    near_a, near_b = None, None
    run_a, run_b = state, factor
    shift = 1
    while shift < span_count:
        last = 2 * shift >= span_count
        if last:
            far = from_behind(run_a, "ctx", direction * shift)
            far_a, far_b = far, None
        else:
            far = from_behind(pack_state(run_a, factor=run_b), "ctx", direction * shift)
            far_a, far_b = far[:, :channels], far[:, channels, :]
        if near_a is None:
            near_a, near_b = far_a, far_b
        else:
            near_a = far_a * near_b[..., None] + near_a
            near_b = None if last else far_b * near_b
        if not last:
            run_a = far_a * run_b[..., None] + run_a
            run_b = far_b * run_b
        shift *= 2
    if near_a is None:
        return jnp.zeros_like(state)
    return near_a


def running_sum(values):
    length = values.shape[0]
    positions = jnp.arange(length, dtype=jnp.int32)
    lower = (positions[:, None] >= positions[None, :]).astype(values.dtype)
    return jnp.einsum("ts,shc->thc", lower, values, precision=lax.Precision.HIGHEST)


def log_decay(logit_in, bias_in):
    return jax.nn.log_sigmoid(logit_in + bias_in) / gate_scale


def segment_ids(start_flags):
    return jnp.cumsum(start_flags, axis=0, dtype=jnp.int32)


def block_inner(query_in, key_in, value_in, logit_in, bias_in, start_flags, kind_id):
    block_len = query_in.shape[0]
    channels = query_in.shape[2]
    log_cum = running_sum(log_decay(logit_in, bias_in))
    segment = segment_ids(start_flags)
    alive_mask = (segment == 0).astype(jnp.float32)
    offsets = jnp.arange(block_len, dtype=jnp.int32)
    distance = offsets[:, None] - offsets[None, :]
    window = block_len // jnp.left_shift(jnp.ones_like(kind_id), kind_id)
    live_pairs = (
        (segment[:, None] == segment[None, :]) & (distance >= 0) & (distance < window)
    )
    query_dec = query_in * jnp.exp(log_cum) * channels ** (-0.5)
    key_dec = key_in * jnp.exp(-log_cum)
    scores = jnp.einsum("ihc,jhc->hij", query_dec, key_dec, precision=highest)
    block_probs = jnp.where(live_pairs[None], scores, 0.0).astype(jnp.bfloat16)
    inner_part = jnp.einsum(
        "hij,jhd->ihd",
        block_probs,
        value_in.astype(jnp.bfloat16),
        preferred_element_type=jnp.float32,
    )
    carried = query_dec * alive_mask[:, None, None]
    return inner_part, carried


def block_summary(key_in, value_in, logit_in, bias_in, start_flags):
    log_cum = running_sum(log_decay(logit_in, bias_in))
    log_last = log_cum[-1]
    segment = segment_ids(start_flags)
    alive_last = (segment[-1] == 0).astype(jnp.float32)
    tail_mask = (segment == segment[-1]).astype(jnp.float32)
    key_tail = key_in * jnp.exp(log_last[None] - log_cum) * tail_mask[:, None, None]
    block_state = jnp.einsum("jhc,jhd->hcd", key_tail, value_in, precision=highest)
    block_decay = jnp.exp(log_last) * alive_last
    return block_state, block_decay


def on_device(
    queries,
    per_head_keys,
    value_rows,
    gate_logits,
    gate_bias,
    value_weight,
    targets,
    mask_ids,
    segment_starts,
):
    token_count = queries.shape[1]
    head_count = gate_bias.shape[0] // DK
    assert mask_ids.shape[1] == 1

    def to_heads(array):
        return array[0].reshape(token_count, head_count, -1).astype(jnp.float32)

    start_flags = segment_starts[0]
    kind_id = mask_ids[0, 0]
    rows_in = lax.optimization_barrier(
        jnp.concatenate([queries, per_head_keys, value_rows, gate_logits], axis=0)
    )
    query_f = to_heads(rows_in[0:1])
    key_f = to_heads(rows_in[1:2])
    value_f = to_heads(rows_in[2:3])
    logit_f = to_heads(rows_in[3:4])
    bias_h = gate_bias.reshape(head_count, DK)

    def inner_terms(query_in, key_in, value_in, logit_in, bias_in):
        return block_inner(query_in, key_in, value_in, logit_in, bias_in, start_flags, kind_id)

    def summary_terms(key_in, value_in, logit_in, bias_in):
        return block_summary(key_in, value_in, logit_in, bias_in, start_flags)

    (attended_local, carried), pull_inner = jax.vjp(
        inner_terms, query_f, key_f, value_f, logit_f, bias_h
    )
    (state_local, decay_local), pull_summary = jax.vjp(
        summary_terms, key_f, value_f, logit_f, bias_h
    )

    span_count = lax.axis_size("ctx")
    state_in = gather_scan(state_local, decay_local, span_count, 1)
    attended = attended_local + jnp.einsum("thc,hcd->thd", carried, state_in, precision=highest)

    def value_head(attended_in, weight_in):
        normed = attended_in * lax.rsqrt(
            jnp.mean(attended_in * attended_in, axis=-1, keepdims=True) + epsilon
        )
        return jnp.einsum("thd,hd->t", normed, weight_in, precision=highest)

    partial_value, pull_value = jax.vjp(value_head, attended, value_weight.reshape(head_count, DV))
    value_pred = butterfly_sum(partial_value, "head")
    residual = value_pred - targets[0]
    grad_attended, grad_weight = pull_value(residual)
    grad_carried = jnp.einsum("thd,hcd->thc", grad_attended, state_in, precision=highest)
    grad_direct = jnp.einsum("thc,thd->hcd", carried, grad_attended, precision=highest)
    inner_grads = pull_inner((grad_attended, grad_carried))

    grad_state = gather_scan(grad_direct, decay_local, span_count, -1)
    grad_decay = jnp.sum(state_in * grad_state, axis=-1)
    summary_grads = pull_summary((grad_state, grad_decay))

    grad_query = inner_grads[0]
    grad_key = inner_grads[1] + summary_grads[0]
    grad_value = inner_grads[2] + summary_grads[1]
    grad_logit = inner_grads[3] + summary_grads[2]
    grad_bias = inner_grads[4] + summary_grads[3]
    token_total = token_count * lax.axis_size("ctx") * lax.axis_size("rep")
    both_total = direct_sum(
        butterfly_sum(jnp.concatenate([grad_bias.reshape(-1), grad_weight.reshape(-1)]), "rep"),
        "ctx",
    )
    bias_total, weight_total = jnp.split(both_total, 2)

    def to_rows(array):
        return array.reshape(1, token_count, -1).astype(jnp.bfloat16)

    return (
        value_pred[None],
        to_rows(grad_query),
        to_rows(grad_key),
        to_rows(grad_value),
        to_rows(grad_logit),
        bias_total / token_total,
        weight_total / token_total,
    )


def solution(mesh):
    in_specs = (
        P(("groups", "rep"), "ctx", "head"),
        P(("groups", "rep"), "ctx", "head"),
        P(("groups", "rep"), "ctx", "head"),
        P(("groups", "rep"), "ctx", "head"),
        P("head"),
        P("head"),
        P(("groups", "rep"), "ctx"),
        P(("groups", "rep"), "ctx"),
        P(("groups", "rep"), "ctx"),
    )
    out_specs = (
        P(("groups", "rep"), "ctx"),
        P(("groups", "rep"), "ctx", "head"),
        P(("groups", "rep"), "ctx", "head"),
        P(("groups", "rep"), "ctx", "head"),
        P(("groups", "rep"), "ctx", "head"),
        P(("groups", "head")),
        P(("groups", "head")),
    )
    return jax.shard_map(
        on_device, mesh=mesh, in_specs=in_specs, out_specs=out_specs, check_vma=False
    )
```

```python
import jax
import jax.numpy as jnp
from jax import lax
from jax.sharding import PartitionSpec as P

DK = 128
DV = 128


epsilon = 1.0
gate_scale = 16.0
highest = lax.Precision.HIGH


def from_behind(value, axis, by):
    length = lax.axis_size(axis)
    pairs = [(i, i + by) for i in range(length) if 0 <= i + by < length]
    return lax.ppermute(value, axis, pairs)


def butterfly_sum(value, axis):
    length = lax.axis_size(axis)
    if length & (length - 1):
        return lax.psum(value, axis)
    bit = 1
    while bit < length:
        pairs = [(i, i ^ bit) for i in range(length)]
        value = value + lax.ppermute(value, axis, pairs)
        bit *= 2
    return value


def direct_sum(value, axis):
    length = lax.axis_size(axis)
    me = lax.axis_index(axis)
    terms = [value]
    for shift in range(1, length):
        pairs = [(i, (i + shift) % length) for i in range(length)]
        terms.append(lax.ppermute(value, axis, pairs))
    def from_member(member):
        source_shift = (me - member) % length
        picked = jnp.zeros_like(value)
        for shift, term in enumerate(terms):
            picked = jnp.where(source_shift == shift, term, picked)
        return picked

    total = from_member(0)
    for member in range(1, length):
        total = total + from_member(member)
    return total


def pack_state(state, factor):
    rows = jnp.zeros((state.shape[0], 8, state.shape[2]), state.dtype)
    rows = rows.at[:, 0, :].set(factor)
    return jnp.concatenate([state, rows], axis=1)


def gather_scan(state, factor, span_count, direction):
    channels = state.shape[1]
    near_a, near_b = None, None
    run_a, run_b = state, factor
    shift = 1
    while shift < span_count:
        last = 2 * shift >= span_count
        if last:
            far = from_behind(run_a, "ctx", direction * shift)
            far_a, far_b = far, None
        else:
            far = from_behind(pack_state(run_a, factor=run_b), "ctx", direction * shift)
            far_a, far_b = far[:, :channels], far[:, channels, :]
        if near_a is None:
            near_a, near_b = far_a, far_b
        else:
            near_a = far_a * near_b[..., None] + near_a
            near_b = None if last else far_b * near_b
        if not last:
            run_a = far_a * run_b[..., None] + run_a
            run_b = far_b * run_b
        shift *= 2
    if near_a is None:
        return jnp.zeros_like(state)
    return near_a


def log_decay(logit_in, bias_in):
    return jax.nn.log_sigmoid(logit_in + bias_in) / gate_scale


def segment_ids(start_flags):
    return jnp.cumsum(start_flags, axis=0, dtype=jnp.int32)


def block_inner(query_in, key_in, value_in, log_cum, start_flags, kind_id):
    block_len = query_in.shape[0]
    channels = query_in.shape[2]
    segment = segment_ids(start_flags)
    alive_mask = (segment == 0).astype(jnp.float32)
    offsets = jnp.arange(block_len, dtype=jnp.int32)
    distance = offsets[:, None] - offsets[None, :]
    window = block_len // jnp.left_shift(jnp.ones_like(kind_id), kind_id)
    live_pairs = (
        (segment[:, None] == segment[None, :]) & (distance >= 0) & (distance < window)
    )
    query_dec = query_in * jnp.exp(log_cum) * channels ** (-0.5)
    key_dec = key_in * jnp.exp(-log_cum)
    scores = jnp.einsum("ihc,jhc->hij", query_dec, key_dec, precision=highest)
    block_probs = jnp.where(live_pairs[None], scores, 0.0).astype(jnp.bfloat16)
    inner_part = jnp.einsum(
        "hij,jhd->ihd",
        block_probs,
        value_in.astype(jnp.bfloat16),
        preferred_element_type=jnp.float32,
    )
    carried = query_dec * alive_mask[:, None, None]
    return inner_part, carried


def block_summary(key_in, value_in, log_cum, start_flags):
    log_last = log_cum[-1]
    segment = segment_ids(start_flags)
    alive_last = (segment[-1] == 0).astype(jnp.float32)
    tail_mask = (segment == segment[-1]).astype(jnp.float32)
    key_tail = key_in * jnp.exp(log_last[None] - log_cum) * tail_mask[:, None, None]
    block_state = jnp.einsum("jhc,jhd->hcd", key_tail, value_in, precision=highest)
    block_decay = jnp.exp(log_last) * alive_last
    return block_state, block_decay


def on_device(
    queries,
    per_head_keys,
    value_rows,
    gate_logits,
    gate_bias,
    value_weight,
    targets,
    mask_ids,
    segment_starts,
):
    token_count = queries.shape[1]
    head_count = gate_bias.shape[0] // DK
    assert mask_ids.shape[1] == 1

    def to_heads(array):
        return array[0].reshape(token_count, head_count, -1).astype(jnp.float32)

    start_flags = segment_starts[0]
    kind_id = mask_ids[0, 0]
    rows_in = lax.optimization_barrier(
        jnp.concatenate([queries, per_head_keys, value_rows, gate_logits], axis=0)
    )
    query_f = to_heads(rows_in[0:1])
    key_f = to_heads(rows_in[1:2])
    value_f = to_heads(rows_in[2:3])
    logit_f = to_heads(rows_in[3:4])
    bias_h = gate_bias.reshape(head_count, DK)

    def inner_terms(query_in, key_in, value_in, log_cum):
        return block_inner(query_in, key_in, value_in, log_cum, start_flags, kind_id)

    def summary_terms(key_in, value_in, log_cum):
        return block_summary(key_in, value_in, log_cum, start_flags)

    def running_decay(logit_in, bias_in):
        return jnp.cumsum(log_decay(logit_in, bias_in), axis=0)

    log_cum, pull_decay = jax.vjp(running_decay, logit_f, bias_h)
    (attended_local, carried), pull_inner = jax.vjp(inner_terms, query_f, key_f, value_f, log_cum)
    (state_local, decay_local), pull_summary = jax.vjp(summary_terms, key_f, value_f, log_cum)

    span_count = lax.axis_size("ctx")
    state_in = gather_scan(state_local, decay_local, span_count, 1)
    attended = attended_local + jnp.einsum("thc,hcd->thd", carried, state_in, precision=highest)

    def value_head(attended_in, weight_in):
        normed = attended_in * lax.rsqrt(
            jnp.mean(attended_in * attended_in, axis=-1, keepdims=True) + epsilon
        )
        return jnp.einsum("thd,hd->t", normed, weight_in, precision=highest)

    partial_value, pull_value = jax.vjp(value_head, attended, value_weight.reshape(head_count, DV))
    value_pred = butterfly_sum(partial_value, "head")
    residual = value_pred - targets[0]
    grad_attended, grad_weight = pull_value(residual)
    grad_carried = jnp.einsum("thd,hcd->thc", grad_attended, state_in, precision=highest)
    grad_direct = jnp.einsum("thc,thd->hcd", carried, grad_attended, precision=highest)
    inner_grads = pull_inner((grad_attended, grad_carried))

    grad_state = gather_scan(grad_direct, decay_local, span_count, -1)
    grad_decay = jnp.sum(state_in * grad_state, axis=-1)
    summary_grads = pull_summary((grad_state, grad_decay))

    grad_logit, grad_bias = pull_decay(inner_grads[3] + summary_grads[2])
    grad_query = inner_grads[0]
    grad_key = inner_grads[1] + summary_grads[0]
    grad_value = inner_grads[2] + summary_grads[1]
    token_total = token_count * lax.axis_size("ctx") * lax.axis_size("rep")
    both_total = direct_sum(
        butterfly_sum(jnp.concatenate([grad_bias.reshape(-1), grad_weight.reshape(-1)]), "rep"),
        "ctx",
    )
    bias_total, weight_total = jnp.split(both_total, 2)

    def to_rows(array):
        return array.reshape(1, token_count, -1).astype(jnp.bfloat16)

    return (
        value_pred[None],
        to_rows(grad_query),
        to_rows(grad_key),
        to_rows(grad_value),
        to_rows(grad_logit),
        bias_total / token_total,
        weight_total / token_total,
    )


def solution(mesh):
    in_specs = (
        P(("groups", "rep"), "ctx", "head"),
        P(("groups", "rep"), "ctx", "head"),
        P(("groups", "rep"), "ctx", "head"),
        P(("groups", "rep"), "ctx", "head"),
        P("head"),
        P("head"),
        P(("groups", "rep"), "ctx"),
        P(("groups", "rep"), "ctx"),
        P(("groups", "rep"), "ctx"),
    )
    out_specs = (
        P(("groups", "rep"), "ctx"),
        P(("groups", "rep"), "ctx", "head"),
        P(("groups", "rep"), "ctx", "head"),
        P(("groups", "rep"), "ctx", "head"),
        P(("groups", "rep"), "ctx", "head"),
        P(("groups", "head")),
        P(("groups", "head")),
    )
    return jax.shard_map(
        on_device, mesh=mesh, in_specs=in_specs, out_specs=out_specs, check_vma=False
    )
```

```python
import jax
import jax.numpy as jnp
from jax import lax
from jax.sharding import PartitionSpec as P

DK = 128
DV = 128


epsilon = 1.0
gate_scale = 16.0
highest = lax.Precision.HIGH


def from_behind(value, axis, by):
    length = lax.axis_size(axis)
    pairs = [(i, i + by) for i in range(length) if 0 <= i + by < length]
    return lax.ppermute(value, axis, pairs)


def butterfly_sum(value, axis):
    length = lax.axis_size(axis)
    if length & (length - 1):
        return lax.psum(value, axis)
    bit = 1
    while bit < length:
        pairs = [(i, i ^ bit) for i in range(length)]
        value = value + lax.ppermute(value, axis, pairs)
        bit *= 2
    return value


def direct_sum(value, axis):
    length = lax.axis_size(axis)
    me = lax.axis_index(axis)
    terms = [value]
    for shift in range(1, length):
        pairs = [(i, (i + shift) % length) for i in range(length)]
        terms.append(lax.ppermute(value, axis, pairs))
    def from_member(member):
        source_shift = (me - member) % length
        picked = jnp.zeros_like(value)
        for shift, term in enumerate(terms):
            picked = jnp.where(source_shift == shift, term, picked)
        return picked

    total = from_member(0)
    for member in range(1, length):
        total = total + from_member(member)
    return total


def factor_runs(factor, span_count, direction):
    runs = []
    run_b = factor
    shift = 1
    while 2 * shift < span_count:
        far_b = from_behind(run_b, "ctx", direction * shift)
        runs.append(far_b)
        run_b = far_b * run_b
        shift *= 2
    return runs


def gather_scan(state, factor, span_count, direction, far_factors):
    near_a, near_b = None, None
    run_a, run_b = state, factor
    shift = 1
    round_index = 0
    while shift < span_count:
        last = 2 * shift >= span_count
        far_a = from_behind(run_a, "ctx", direction * shift)
        far_b = None if last else far_factors[round_index]
        if near_a is None:
            near_a, near_b = far_a, far_b
        else:
            near_a = far_a * near_b[..., None] + near_a
            near_b = None if last else far_b * near_b
        if not last:
            run_a = far_a * run_b[..., None] + run_a
            run_b = far_b * run_b
        shift *= 2
        round_index += 1
    if near_a is None:
        return jnp.zeros_like(state)
    return near_a


def log_decay(logit_in, bias_in):
    return jax.nn.log_sigmoid(logit_in + bias_in) / gate_scale


def segment_ids(start_flags):
    return jnp.cumsum(start_flags, axis=0, dtype=jnp.int32)


def block_inner(query_in, key_in, value_in, logit_in, bias_in, start_flags, kind_id):
    block_len = query_in.shape[0]
    channels = query_in.shape[2]
    log_cum = jnp.cumsum(log_decay(logit_in, bias_in), axis=0)
    segment = segment_ids(start_flags)
    alive_mask = (segment == 0).astype(jnp.float32)
    offsets = jnp.arange(block_len, dtype=jnp.int32)
    distance = offsets[:, None] - offsets[None, :]
    window = block_len // jnp.left_shift(jnp.ones_like(kind_id), kind_id)
    live_pairs = (
        (segment[:, None] == segment[None, :]) & (distance >= 0) & (distance < window)
    )
    query_dec = query_in * jnp.exp(log_cum) * channels ** (-0.5)
    key_dec = key_in * jnp.exp(-log_cum)
    scores = jnp.einsum("ihc,jhc->hij", query_dec, key_dec, precision=highest)
    block_probs = jnp.where(live_pairs[None], scores, 0.0).astype(jnp.bfloat16)
    inner_part = jnp.einsum(
        "hij,jhd->ihd",
        block_probs,
        value_in.astype(jnp.bfloat16),
        preferred_element_type=jnp.float32,
    )
    carried = query_dec * alive_mask[:, None, None]
    return inner_part, carried


def block_summary(key_in, value_in, logit_in, bias_in, start_flags):
    log_cum = jnp.cumsum(log_decay(logit_in, bias_in), axis=0)
    log_last = log_cum[-1]
    segment = segment_ids(start_flags)
    alive_last = (segment[-1] == 0).astype(jnp.float32)
    tail_mask = (segment == segment[-1]).astype(jnp.float32)
    key_tail = key_in * jnp.exp(log_last[None] - log_cum) * tail_mask[:, None, None]
    block_state = jnp.einsum("jhc,jhd->hcd", key_tail, value_in, precision=highest)
    block_decay = jnp.exp(log_last) * alive_last
    return block_state, block_decay


def on_device(
    queries,
    per_head_keys,
    value_rows,
    gate_logits,
    gate_bias,
    value_weight,
    targets,
    mask_ids,
    segment_starts,
):
    token_count = queries.shape[1]
    head_count = gate_bias.shape[0] // DK
    assert mask_ids.shape[1] == 1

    def to_heads(array):
        return array[0].reshape(token_count, head_count, -1).astype(jnp.float32)

    start_flags = segment_starts[0]
    kind_id = mask_ids[0, 0]
    rows_in = lax.optimization_barrier(
        jnp.concatenate([queries, per_head_keys, value_rows, gate_logits], axis=0)
    )
    query_f = to_heads(rows_in[0:1])
    key_f = to_heads(rows_in[1:2])
    value_f = to_heads(rows_in[2:3])
    logit_f = to_heads(rows_in[3:4])
    bias_h = gate_bias.reshape(head_count, DK)

    def inner_terms(query_in, key_in, value_in, logit_in, bias_in):
        return block_inner(query_in, key_in, value_in, logit_in, bias_in, start_flags, kind_id)

    def summary_terms(key_in, value_in, logit_in, bias_in):
        return block_summary(key_in, value_in, logit_in, bias_in, start_flags)

    (attended_local, carried), pull_inner = jax.vjp(
        inner_terms, query_f, key_f, value_f, logit_f, bias_h
    )
    (state_local, decay_local), pull_summary = jax.vjp(
        summary_terms, key_f, value_f, logit_f, bias_h
    )

    span_count = lax.axis_size("ctx")
    forward_runs = factor_runs(decay_local, span_count, 1)
    backward_runs = factor_runs(decay_local, span_count, -1)
    state_in = gather_scan(state_local, decay_local, span_count, 1, forward_runs)
    attended = attended_local + jnp.einsum("thc,hcd->thd", carried, state_in, precision=highest)

    def value_head(attended_in, weight_in):
        normed = attended_in * lax.rsqrt(
            jnp.mean(attended_in * attended_in, axis=-1, keepdims=True) + epsilon
        )
        return jnp.einsum("thd,hd->t", normed, weight_in, precision=highest)

    partial_value, pull_value = jax.vjp(value_head, attended, value_weight.reshape(head_count, DV))
    value_pred = butterfly_sum(partial_value, "head")
    residual = value_pred - targets[0]
    grad_attended, grad_weight = pull_value(residual)
    grad_carried = jnp.einsum("thd,hcd->thc", grad_attended, state_in, precision=highest)
    grad_direct = jnp.einsum("thc,thd->hcd", carried, grad_attended, precision=highest)
    inner_grads = pull_inner((grad_attended, grad_carried))

    grad_state = gather_scan(grad_direct, decay_local, span_count, -1, backward_runs)
    grad_decay = jnp.sum(state_in * grad_state, axis=-1)
    summary_grads = pull_summary((grad_state, grad_decay))

    grad_query = inner_grads[0]
    grad_key = inner_grads[1] + summary_grads[0]
    grad_value = inner_grads[2] + summary_grads[1]
    grad_logit = inner_grads[3] + summary_grads[2]
    grad_bias = inner_grads[4] + summary_grads[3]
    token_total = token_count * lax.axis_size("ctx") * lax.axis_size("rep")
    both_total = direct_sum(
        butterfly_sum(jnp.concatenate([grad_bias.reshape(-1), grad_weight.reshape(-1)]), "rep"),
        "ctx",
    )
    bias_total, weight_total = jnp.split(both_total, 2)

    def to_rows(array):
        return array.reshape(1, token_count, -1).astype(jnp.bfloat16)

    return (
        value_pred[None],
        to_rows(grad_query),
        to_rows(grad_key),
        to_rows(grad_value),
        to_rows(grad_logit),
        bias_total / token_total,
        weight_total / token_total,
    )


def solution(mesh):
    in_specs = (
        P(("groups", "rep"), "ctx", "head"),
        P(("groups", "rep"), "ctx", "head"),
        P(("groups", "rep"), "ctx", "head"),
        P(("groups", "rep"), "ctx", "head"),
        P("head"),
        P("head"),
        P(("groups", "rep"), "ctx"),
        P(("groups", "rep"), "ctx"),
        P(("groups", "rep"), "ctx"),
    )
    out_specs = (
        P(("groups", "rep"), "ctx"),
        P(("groups", "rep"), "ctx", "head"),
        P(("groups", "rep"), "ctx", "head"),
        P(("groups", "rep"), "ctx", "head"),
        P(("groups", "rep"), "ctx", "head"),
        P(("groups", "head")),
        P(("groups", "head")),
    )
    return jax.shard_map(
        on_device, mesh=mesh, in_specs=in_specs, out_specs=out_specs, check_vma=False
    )
```

```python
import jax
import jax.numpy as jnp
from jax import lax
from jax.sharding import PartitionSpec as P

DK = 128
DV = 128


epsilon = 1.0
gate_scale = 16.0
highest = lax.Precision.HIGH


def from_behind(value, axis, by):
    length = lax.axis_size(axis)
    pairs = [(i, i + by) for i in range(length) if 0 <= i + by < length]
    return lax.ppermute(value, axis, pairs)


def butterfly_sum(value, axis):
    length = lax.axis_size(axis)
    if length & (length - 1):
        return lax.psum(value, axis)
    bit = 1
    while bit < length:
        pairs = [(i, i ^ bit) for i in range(length)]
        value = value + lax.ppermute(value, axis, pairs)
        bit *= 2
    return value


def direct_sum(value, axis):
    length = lax.axis_size(axis)
    me = lax.axis_index(axis)
    terms = [value]
    for shift in range(1, length):
        pairs = [(i, (i + shift) % length) for i in range(length)]
        terms.append(lax.ppermute(value, axis, pairs))
    def from_member(member):
        source_shift = (me - member) % length
        picked = jnp.zeros_like(value)
        for shift, term in enumerate(terms):
            picked = jnp.where(source_shift == shift, term, picked)
        return picked

    total = from_member(0)
    for member in range(1, length):
        total = total + from_member(member)
    return total


def pack_state(state, factor):
    rows = jnp.zeros((state.shape[0], 8, state.shape[2]), state.dtype)
    rows = rows.at[:, 0, :].set(factor)
    return jnp.concatenate([state, rows], axis=1)


def gather_scan(state, factor, span_count, direction):
    channels = state.shape[1]
    near_a, near_b = None, None
    run_a, run_b = state, factor
    shift = 1
    while shift < span_count:
        last = 2 * shift >= span_count
        if last:
            far = from_behind(run_a, "ctx", direction * shift)
            far_a, far_b = far, None
        else:
            far = from_behind(pack_state(run_a, factor=run_b), "ctx", direction * shift)
            far_a, far_b = far[:, :channels], far[:, channels, :]
        if near_a is None:
            near_a, near_b = far_a, far_b
        else:
            near_a = far_a * near_b[..., None] + near_a
            near_b = None if last else far_b * near_b
        if not last:
            run_a = far_a * run_b[..., None] + run_a
            run_b = far_b * run_b
        shift *= 2
    if near_a is None:
        return jnp.zeros_like(state)
    return near_a


def log_decay(logit_in, bias_in):
    return jax.nn.log_sigmoid(logit_in + bias_in) / gate_scale


def segment_ids(start_flags):
    return jnp.cumsum(start_flags, axis=0, dtype=jnp.int32)


def block_inner(query_in, key_in, value_in, logit_in, bias_in, start_flags, kind_id):
    block_len = query_in.shape[0]
    channels = query_in.shape[2]
    log_cum = jnp.cumsum(log_decay(logit_in, bias_in), axis=0)
    segment = segment_ids(start_flags)
    alive_mask = (segment == 0).astype(jnp.float32)
    offsets = jnp.arange(block_len, dtype=jnp.int32)
    distance = offsets[:, None] - offsets[None, :]
    window = block_len // jnp.left_shift(jnp.ones_like(kind_id), kind_id)
    live_pairs = (
        (segment[:, None] == segment[None, :]) & (distance >= 0) & (distance < window)
    )
    query_dec = query_in * jnp.exp(log_cum) * channels ** (-0.5)
    key_dec = key_in * jnp.exp(-log_cum)
    scores = jnp.einsum("ihc,jhc->hij", query_dec, key_dec, precision=highest)
    block_probs = jnp.where(live_pairs[None], scores, 0.0).astype(jnp.bfloat16)
    inner_part = jnp.einsum(
        "hij,jhd->ihd",
        block_probs,
        value_in.astype(jnp.bfloat16),
        preferred_element_type=jnp.float32,
    )
    carried = query_dec * alive_mask[:, None, None]
    return inner_part, carried


def block_summary(key_in, value_in, logit_in, bias_in, start_flags):
    log_cum = jnp.cumsum(log_decay(logit_in, bias_in), axis=0)
    log_last = log_cum[-1]
    segment = segment_ids(start_flags)
    last_segment = jnp.sum(start_flags)
    alive_last = (last_segment == 0).astype(jnp.float32)
    tail_mask = (segment == last_segment).astype(jnp.float32)
    key_tail = key_in * jnp.exp(log_last[None] - log_cum) * tail_mask[:, None, None]
    block_state = jnp.einsum("jhc,jhd->hcd", key_tail, value_in, precision=highest)
    block_decay = jnp.exp(log_last) * alive_last
    return block_state, block_decay


def on_device(
    queries,
    per_head_keys,
    value_rows,
    gate_logits,
    gate_bias,
    value_weight,
    targets,
    mask_ids,
    segment_starts,
):
    token_count = queries.shape[1]
    head_count = gate_bias.shape[0] // DK
    assert mask_ids.shape[1] == 1

    def to_heads(array):
        return array[0].reshape(token_count, head_count, -1).astype(jnp.float32)

    start_flags = segment_starts[0]
    kind_id = mask_ids[0, 0]
    rows_in = lax.optimization_barrier(
        jnp.concatenate([queries, per_head_keys, value_rows, gate_logits], axis=0)
    )
    query_f = to_heads(rows_in[0:1])
    key_f = to_heads(rows_in[1:2])
    value_f = to_heads(rows_in[2:3])
    logit_f = to_heads(rows_in[3:4])
    bias_h = gate_bias.reshape(head_count, DK)

    def inner_terms(query_in, key_in, value_in, logit_in, bias_in):
        return block_inner(query_in, key_in, value_in, logit_in, bias_in, start_flags, kind_id)

    def summary_terms(key_in, value_in, logit_in, bias_in):
        return block_summary(key_in, value_in, logit_in, bias_in, start_flags)

    (attended_local, carried), pull_inner = jax.vjp(
        inner_terms, query_f, key_f, value_f, logit_f, bias_h
    )
    (state_local, decay_local), pull_summary = jax.vjp(
        summary_terms, key_f, value_f, logit_f, bias_h
    )

    span_count = lax.axis_size("ctx")
    state_in = gather_scan(state_local, decay_local, span_count, 1)
    attended = attended_local + jnp.einsum("thc,hcd->thd", carried, state_in, precision=highest)

    def value_head(attended_in, weight_in):
        normed = attended_in * lax.rsqrt(
            jnp.mean(attended_in * attended_in, axis=-1, keepdims=True) + epsilon
        )
        return jnp.einsum("thd,hd->t", normed, weight_in, precision=highest)

    partial_value, pull_value = jax.vjp(value_head, attended, value_weight.reshape(head_count, DV))
    value_pred = butterfly_sum(partial_value, "head")
    residual = value_pred - targets[0]
    grad_attended, grad_weight = pull_value(residual)
    grad_carried = jnp.einsum("thd,hcd->thc", grad_attended, state_in, precision=highest)
    grad_direct = jnp.einsum("thc,thd->hcd", carried, grad_attended, precision=highest)
    inner_grads = pull_inner((grad_attended, grad_carried))

    grad_state = gather_scan(grad_direct, decay_local, span_count, -1)
    grad_decay = jnp.sum(state_in * grad_state, axis=-1)
    summary_grads = pull_summary((grad_state, grad_decay))

    grad_query = inner_grads[0]
    grad_key = inner_grads[1] + summary_grads[0]
    grad_value = inner_grads[2] + summary_grads[1]
    grad_logit = inner_grads[3] + summary_grads[2]
    grad_bias = inner_grads[4] + summary_grads[3]
    token_total = token_count * lax.axis_size("ctx") * lax.axis_size("rep")
    both_total = direct_sum(
        butterfly_sum(jnp.concatenate([grad_bias.reshape(-1), grad_weight.reshape(-1)]), "rep"),
        "ctx",
    )
    bias_total, weight_total = jnp.split(both_total, 2)

    def to_rows(array):
        return array.reshape(1, token_count, -1).astype(jnp.bfloat16)

    return (
        value_pred[None],
        to_rows(grad_query),
        to_rows(grad_key),
        to_rows(grad_value),
        to_rows(grad_logit),
        bias_total / token_total,
        weight_total / token_total,
    )


def solution(mesh):
    in_specs = (
        P(("groups", "rep"), "ctx", "head"),
        P(("groups", "rep"), "ctx", "head"),
        P(("groups", "rep"), "ctx", "head"),
        P(("groups", "rep"), "ctx", "head"),
        P("head"),
        P("head"),
        P(("groups", "rep"), "ctx"),
        P(("groups", "rep"), "ctx"),
        P(("groups", "rep"), "ctx"),
    )
    out_specs = (
        P(("groups", "rep"), "ctx"),
        P(("groups", "rep"), "ctx", "head"),
        P(("groups", "rep"), "ctx", "head"),
        P(("groups", "rep"), "ctx", "head"),
        P(("groups", "rep"), "ctx", "head"),
        P(("groups", "head")),
        P(("groups", "head")),
    )
    return jax.shard_map(
        on_device, mesh=mesh, in_specs=in_specs, out_specs=out_specs, check_vma=False
    )
```

```python
import jax
import jax.numpy as jnp
from jax import lax
from jax.sharding import PartitionSpec as P

DK = 128
DV = 128


epsilon = 1.0
gate_scale = 16.0
highest = lax.Precision.HIGH


def from_behind(value, axis, by):
    length = lax.axis_size(axis)
    pairs = [(i, i + by) for i in range(length) if 0 <= i + by < length]
    return lax.ppermute(value, axis, pairs)


def butterfly_sum(value, axis):
    length = lax.axis_size(axis)
    if length & (length - 1):
        return lax.psum(value, axis)
    bit = 1
    while bit < length:
        pairs = [(i, i ^ bit) for i in range(length)]
        value = value + lax.ppermute(value, axis, pairs)
        bit *= 2
    return value


def direct_sum(value, axis):
    length = lax.axis_size(axis)
    me = lax.axis_index(axis)
    terms = [value]
    for shift in range(1, length):
        pairs = [(i, (i + shift) % length) for i in range(length)]
        terms.append(lax.ppermute(value, axis, pairs))
    def from_member(member):
        source_shift = (me - member) % length
        picked = jnp.zeros_like(value)
        for shift, term in enumerate(terms):
            picked = jnp.where(source_shift == shift, term, picked)
        return picked

    total = from_member(0)
    for member in range(1, length):
        total = total + from_member(member)
    return total


def pack_state(state, factor):
    rows = jnp.zeros((state.shape[0], 8, state.shape[2]), state.dtype)
    rows = rows.at[:, 0, :].set(factor)
    return jnp.concatenate([state, rows], axis=1)


def gather_scan(state, factor, span_count, direction):
    channels = state.shape[1]
    near_a, near_b = None, None
    run_a, run_b = state, factor
    shift = 1
    while shift < span_count:
        last = 2 * shift >= span_count
        if last:
            far = from_behind(run_a, "ctx", direction * shift)
            far_a, far_b = far, None
        else:
            far = from_behind(pack_state(run_a, factor=run_b), "ctx", direction * shift)
            far_a, far_b = far[:, :channels], far[:, channels, :]
        if near_a is None:
            near_a, near_b = far_a, far_b
        else:
            near_a = far_a * near_b[..., None] + near_a
            near_b = None if last else far_b * near_b
        if not last:
            run_a = far_a * run_b[..., None] + run_a
            run_b = far_b * run_b
        shift *= 2
    if near_a is None:
        return jnp.zeros_like(state)
    return near_a


def log_decay(logit_in, bias_in):
    return jax.nn.log_sigmoid(logit_in + bias_in) / gate_scale


def segment_ids(start_flags):
    return jnp.cumsum(start_flags, axis=0, dtype=jnp.int32)


def block_inner(query_in, key_in, value_in, logit_in, bias_in, start_flags, kind_id):
    block_len = query_in.shape[0]
    channels = query_in.shape[2]
    log_cum = jnp.cumsum(log_decay(logit_in, bias_in), axis=0)
    segment = segment_ids(start_flags)
    alive_mask = (segment == 0).astype(jnp.float32)
    offsets = jnp.arange(block_len, dtype=jnp.int32)
    distance = offsets[:, None] - offsets[None, :]
    window = block_len // jnp.left_shift(jnp.ones_like(kind_id), kind_id)
    live_pairs = (
        (segment[:, None] == segment[None, :]) & (distance >= 0) & (distance < window)
    )
    query_dec = query_in * jnp.exp(log_cum) * channels ** (-0.5)
    key_dec = key_in * jnp.exp(-log_cum)
    scores = jnp.einsum("ihc,jhc->hij", query_dec, key_dec, precision=highest)
    block_probs = jnp.where(live_pairs[None], scores, 0.0).astype(jnp.bfloat16)
    inner_part = jnp.einsum(
        "hij,jhd->ihd",
        block_probs,
        value_in.astype(jnp.bfloat16),
        preferred_element_type=jnp.float32,
    )
    carried = query_dec * alive_mask[:, None, None]
    return inner_part, carried


def block_summary(key_in, value_in, logit_in, bias_in, start_flags):
    log_cum = jnp.cumsum(log_decay(logit_in, bias_in), axis=0)
    log_last = log_cum[-1]
    segment = segment_ids(start_flags)
    alive_last = (segment[-1] == 0).astype(jnp.float32)
    tail_mask = (segment == segment[-1]).astype(jnp.float32)
    key_tail = key_in * jnp.exp(log_last[None] - log_cum) * tail_mask[:, None, None]
    block_state = jnp.einsum("jhc,jhd->hcd", key_tail, value_in, precision=highest)
    block_decay = jnp.exp(log_last) * alive_last
    return block_state, block_decay


def on_device(
    queries,
    per_head_keys,
    value_rows,
    gate_logits,
    gate_bias,
    value_weight,
    targets,
    mask_ids,
    segment_starts,
):
    token_count = queries.shape[1]
    head_count = gate_bias.shape[0] // DK
    assert mask_ids.shape[1] == 1

    def to_heads(array):
        return array[0].reshape(token_count, head_count, -1).astype(jnp.float32)

    start_flags = segment_starts[0]
    kind_id = mask_ids[0, 0]
    rows_in = lax.optimization_barrier(
        jnp.concatenate([per_head_keys, value_rows, gate_logits], axis=0)
    )
    query_f = to_heads(queries)
    key_f = to_heads(rows_in[0:1])
    value_f = to_heads(rows_in[1:2])
    logit_f = to_heads(rows_in[2:3])
    bias_h = gate_bias.reshape(head_count, DK)

    def inner_terms(query_in, key_in, value_in, logit_in, bias_in):
        return block_inner(query_in, key_in, value_in, logit_in, bias_in, start_flags, kind_id)

    def summary_terms(key_in, value_in, logit_in, bias_in):
        return block_summary(key_in, value_in, logit_in, bias_in, start_flags)

    (attended_local, carried), pull_inner = jax.vjp(
        inner_terms, query_f, key_f, value_f, logit_f, bias_h
    )
    (state_local, decay_local), pull_summary = jax.vjp(
        summary_terms, key_f, value_f, logit_f, bias_h
    )

    span_count = lax.axis_size("ctx")
    state_in = gather_scan(state_local, decay_local, span_count, 1)
    attended = attended_local + jnp.einsum("thc,hcd->thd", carried, state_in, precision=highest)

    def value_head(attended_in, weight_in):
        normed = attended_in * lax.rsqrt(
            jnp.mean(attended_in * attended_in, axis=-1, keepdims=True) + epsilon
        )
        return jnp.einsum("thd,hd->t", normed, weight_in, precision=highest)

    partial_value, pull_value = jax.vjp(value_head, attended, value_weight.reshape(head_count, DV))
    value_pred = butterfly_sum(partial_value, "head")
    residual = value_pred - targets[0]
    grad_attended, grad_weight = pull_value(residual)
    grad_carried = jnp.einsum("thd,hcd->thc", grad_attended, state_in, precision=highest)
    grad_direct = jnp.einsum("thc,thd->hcd", carried, grad_attended, precision=highest)
    inner_grads = pull_inner((grad_attended, grad_carried))

    grad_state = gather_scan(grad_direct, decay_local, span_count, -1)
    grad_decay = jnp.sum(state_in * grad_state, axis=-1)
    summary_grads = pull_summary((grad_state, grad_decay))

    grad_query = inner_grads[0]
    grad_key = inner_grads[1] + summary_grads[0]
    grad_value = inner_grads[2] + summary_grads[1]
    grad_logit = inner_grads[3] + summary_grads[2]
    grad_bias = inner_grads[4] + summary_grads[3]
    token_total = token_count * lax.axis_size("ctx") * lax.axis_size("rep")
    both_total = direct_sum(
        butterfly_sum(jnp.concatenate([grad_bias.reshape(-1), grad_weight.reshape(-1)]), "rep"),
        "ctx",
    )
    bias_total, weight_total = jnp.split(both_total, 2)

    def to_rows(array):
        return array.reshape(1, token_count, -1).astype(jnp.bfloat16)

    return (
        value_pred[None],
        to_rows(grad_query),
        to_rows(grad_key),
        to_rows(grad_value),
        to_rows(grad_logit),
        bias_total / token_total,
        weight_total / token_total,
    )


def solution(mesh):
    in_specs = (
        P(("groups", "rep"), "ctx", "head"),
        P(("groups", "rep"), "ctx", "head"),
        P(("groups", "rep"), "ctx", "head"),
        P(("groups", "rep"), "ctx", "head"),
        P("head"),
        P("head"),
        P(("groups", "rep"), "ctx"),
        P(("groups", "rep"), "ctx"),
        P(("groups", "rep"), "ctx"),
    )
    out_specs = (
        P(("groups", "rep"), "ctx"),
        P(("groups", "rep"), "ctx", "head"),
        P(("groups", "rep"), "ctx", "head"),
        P(("groups", "rep"), "ctx", "head"),
        P(("groups", "rep"), "ctx", "head"),
        P(("groups", "head")),
        P(("groups", "head")),
    )
    return jax.shard_map(
        on_device, mesh=mesh, in_specs=in_specs, out_specs=out_specs, check_vma=False
    )
```

```python
import jax
import jax.numpy as jnp
from jax import lax
from jax.sharding import PartitionSpec as P

DK = 128
DV = 128


epsilon = 1.0
gate_scale = 16.0
highest = lax.Precision.HIGH


def from_behind(value, axis, by):
    length = lax.axis_size(axis)
    pairs = [(i, i + by) for i in range(length) if 0 <= i + by < length]
    return lax.ppermute(value, axis, pairs)


def butterfly_sum(value, axis):
    length = lax.axis_size(axis)
    if length & (length - 1):
        return lax.psum(value, axis)
    bit = 1
    while bit < length:
        pairs = [(i, i ^ bit) for i in range(length)]
        value = value + lax.ppermute(value, axis, pairs)
        bit *= 2
    return value


def direct_sum(value, axis):
    length = lax.axis_size(axis)
    me = lax.axis_index(axis)
    terms = [value]
    for shift in range(1, length):
        pairs = [(i, (i + shift) % length) for i in range(length)]
        terms.append(lax.ppermute(value, axis, pairs))
    def from_member(member):
        source_shift = (me - member) % length
        picked = jnp.zeros_like(value)
        for shift, term in enumerate(terms):
            picked = jnp.where(source_shift == shift, term, picked)
        return picked

    total = from_member(0)
    for member in range(1, length):
        total = total + from_member(member)
    return total


def pack_state(state, factor):
    rows = jnp.zeros((state.shape[0], 8, state.shape[2]), state.dtype)
    rows = rows.at[:, 0, :].set(factor)
    return jnp.concatenate([state, rows], axis=1)


def gather_scan(state, factor, span_count, direction):
    channels = state.shape[1]
    near_a, near_b = None, None
    run_a, run_b = state, factor
    shift = 1
    while shift < span_count:
        last = 2 * shift >= span_count
        if last:
            far = from_behind(run_a, "ctx", direction * shift)
            far_a, far_b = far, None
        else:
            far = from_behind(pack_state(run_a, factor=run_b), "ctx", direction * shift)
            far_a, far_b = far[:, :channels], far[:, channels, :]
        if near_a is None:
            near_a, near_b = far_a, far_b
        else:
            near_a = far_a * near_b[..., None] + near_a
            near_b = None if last else far_b * near_b
        if not last:
            run_a = far_a * run_b[..., None] + run_a
            run_b = far_b * run_b
        shift *= 2
    if near_a is None:
        return jnp.zeros_like(state)
    return near_a


def log_decay(logit_in, bias_in):
    return jax.nn.log_sigmoid(logit_in + bias_in) / gate_scale


def segment_ids(start_flags):
    return jnp.cumsum(start_flags, axis=0, dtype=jnp.int32)


def block_inner(query_in, key_in, value_in, logit_in, bias_in, start_flags, kind_id):
    block_len = query_in.shape[0]
    channels = query_in.shape[2]
    log_cum = jnp.cumsum(log_decay(logit_in, bias_in), axis=0)
    segment = segment_ids(start_flags)
    alive_mask = (segment == 0).astype(jnp.float32)
    offsets = jnp.arange(block_len, dtype=jnp.int32)
    distance = offsets[:, None] - offsets[None, :]
    window = block_len // jnp.left_shift(jnp.ones_like(kind_id), kind_id)
    live_pairs = (
        (segment[:, None] == segment[None, :]) & (distance >= 0) & (distance < window)
    )
    query_dec = query_in * jnp.exp(log_cum) * channels ** (-0.5)
    key_dec = key_in * jnp.exp(-log_cum)
    scores = jnp.einsum("ihc,jhc->hij", query_dec, key_dec, precision=highest)
    block_probs = jnp.where(live_pairs[None], scores, 0.0).astype(jnp.bfloat16)
    inner_part = jnp.einsum(
        "hij,jhd->ihd",
        block_probs,
        value_in.astype(jnp.bfloat16),
        preferred_element_type=jnp.float32,
    )
    carried = query_dec * alive_mask[:, None, None]
    return inner_part, carried


def block_summary(key_in, value_in, logit_in, bias_in, start_flags):
    log_cum = jnp.cumsum(log_decay(logit_in, bias_in), axis=0)
    log_last = log_cum[-1]
    segment = segment_ids(start_flags)
    alive_last = (segment[-1] == 0).astype(jnp.float32)
    tail_mask = (segment == segment[-1]).astype(jnp.float32)
    key_tail = key_in * jnp.exp(log_last[None] - log_cum) * tail_mask[:, None, None]
    block_state = jnp.einsum("jhc,jhd->hcd", key_tail, value_in, precision=highest)
    block_decay = jnp.exp(log_last) * alive_last
    return block_state, block_decay


def on_device(
    queries,
    per_head_keys,
    value_rows,
    gate_logits,
    gate_bias,
    value_weight,
    targets,
    mask_ids,
    segment_starts,
):
    token_count = queries.shape[1]
    head_count = gate_bias.shape[0] // DK
    assert mask_ids.shape[1] == 1

    def to_heads(array):
        return array[0].reshape(token_count, head_count, -1).astype(jnp.float32)

    start_flags = segment_starts[0]
    kind_id = mask_ids[0, 0]
    rows_in = lax.optimization_barrier(
        jnp.concatenate([queries, per_head_keys, value_rows, gate_logits], axis=0)
    )
    query_f = to_heads(rows_in[0:1])
    key_f = to_heads(rows_in[1:2])
    value_f = to_heads(rows_in[2:3])
    logit_f = to_heads(rows_in[3:4])
    bias_h = gate_bias.reshape(head_count, DK)

    def inner_terms(query_in, key_in, value_in, logit_in, bias_in):
        return block_inner(query_in, key_in, value_in, logit_in, bias_in, start_flags, kind_id)

    def summary_terms(key_in, value_in, logit_in, bias_in):
        return block_summary(key_in, value_in, logit_in, bias_in, start_flags)

    (attended_local, carried), pull_inner = jax.vjp(
        inner_terms, query_f, key_f, value_f, logit_f, bias_h
    )
    (state_local, decay_local), pull_summary = jax.vjp(
        summary_terms, key_f, value_f, logit_f, bias_h
    )

    span_count = lax.axis_size("ctx")
    state_in = gather_scan(state_local, decay_local, span_count, 1)
    attended = attended_local + jnp.einsum("thc,hcd->thd", carried, state_in, precision=highest)

    def value_head(attended_in, weight_in):
        normed = attended_in * lax.rsqrt(
            jnp.mean(attended_in * attended_in, axis=-1, keepdims=True) + epsilon
        )
        return jnp.einsum("thd,hd->t", normed, weight_in, precision=highest)

    partial_value, pull_value = jax.vjp(value_head, attended, value_weight.reshape(head_count, DV))
    value_pred = butterfly_sum(partial_value, "head")
    residual = value_pred - targets[0]
    grad_attended, grad_weight = pull_value(residual)
    grad_carried = jnp.einsum("thd,hcd->thc", grad_attended, state_in, precision=highest)
    grad_direct = jnp.einsum("thc,thd->hcd", carried, grad_attended, precision=highest)
    inner_grads = pull_inner((grad_attended, grad_carried))

    grad_state = gather_scan(grad_direct, decay_local, span_count, -1)
    grad_decay = jnp.sum(state_in * grad_state, axis=-1)
    summary_grads = pull_summary((grad_state, grad_decay))

    grad_query = inner_grads[0]
    grad_key = inner_grads[1] + summary_grads[0]
    grad_value = inner_grads[2] + summary_grads[1]
    grad_logit = inner_grads[3] + summary_grads[2]
    grad_bias = inner_grads[4] + summary_grads[3]
    token_total = token_count * lax.axis_size("ctx") * lax.axis_size("rep")
    both_total = direct_sum(
        butterfly_sum(
            jnp.concatenate([grad_bias.reshape(-1), grad_weight.reshape(-1)]) / token_total, "rep"
        ),
        "ctx",
    )
    bias_total, weight_total = jnp.split(both_total, 2)

    def to_rows(array):
        return array.reshape(1, token_count, -1).astype(jnp.bfloat16)

    return (
        value_pred[None],
        to_rows(grad_query),
        to_rows(grad_key),
        to_rows(grad_value),
        to_rows(grad_logit),
        bias_total,
        weight_total,
    )


def solution(mesh):
    in_specs = (
        P(("groups", "rep"), "ctx", "head"),
        P(("groups", "rep"), "ctx", "head"),
        P(("groups", "rep"), "ctx", "head"),
        P(("groups", "rep"), "ctx", "head"),
        P("head"),
        P("head"),
        P(("groups", "rep"), "ctx"),
        P(("groups", "rep"), "ctx"),
        P(("groups", "rep"), "ctx"),
    )
    out_specs = (
        P(("groups", "rep"), "ctx"),
        P(("groups", "rep"), "ctx", "head"),
        P(("groups", "rep"), "ctx", "head"),
        P(("groups", "rep"), "ctx", "head"),
        P(("groups", "rep"), "ctx", "head"),
        P(("groups", "head")),
        P(("groups", "head")),
    )
    return jax.shard_map(
        on_device, mesh=mesh, in_specs=in_specs, out_specs=out_specs, check_vma=False
    )
```
